512 devices in a mesh: row: 16 (over x, y), ch: 32 (over z, core).
Axes of the slice: x: 4, y: 4, z: 16, core: 2. Of those that a mesh axis runs over, the one named last changes fastest.
Arguments:
- features: bfloat16 [16, 256, 4096], P('row', None, 'ch'), may hold values from -6 to 6
- w_in: bfloat16 [4096, 4096], P(None, 'ch'), may hold values from -0.1875 to 0.1875
- w_group: bfloat16 [3, 3, 64, 4096], P(None, None, None, 'ch'), may hold values from -0.25 to 0.25
- w_out: bfloat16 [4096, 4096], P(None, 'ch'), may hold values from -0.1875 to 0.1875
- cotangent: bfloat16 [16, 256, 4096], P('row', None, 'ch'), may hold values from -6 to 6
Outputs:
- block_out: bfloat16 [16, 256, 4096], P('row', None, 'ch')
- grad_input: bfloat16 [16, 256, 4096], P('row', None, 'ch')
- grad_w_in: bfloat16 [4096, 4096], P(None, 'ch')
- grad_w_group: bfloat16 [3, 3, 64, 4096], P(None, None, None, 'ch')
- grad_w_out: bfloat16 [4096, 4096], P(None, 'ch')
The draws below stay inside these ranges and needn't reach their ends.
All inputs are finite; a program needn't handle non-finite values.
Results may differ from the reference program's by a relative error of at most 0.017.
Values may be sent and summed in bfloat16 or wider, within the bound.
No kernel may reach another device: no remote copies, remote signals or barrier semaphores. Data moves between devices by JAX's collectives and lax.ppermute only.
A program may use at most 64 MiB of HBM per device.

```python
import jax
import jax.numpy as jnp
from jax import lax

C = 4096
M = 4096
GW = 64
ROW_DEV = 1
COLS = 256
GROUPS = 64
HEIGHT = 16
N_ROW = 16
N_CH = 32


def with_spikes(values, stream_key, source, target, blocks, factor):
    def block_of(axis_at):
        return (jnp.arange(values.shape[axis_at]) // (values.shape[axis_at] // blocks)).reshape((-1,) + (1,) * (values.ndim - 1 - axis_at))

    near = jax.random.permutation(stream_key, blocks)[block_of(target)]
    other_side = (block_of(target) + blocks // 2) % blocks
    return jnp.where((block_of(source) == near) | (block_of(source) == other_side), factor * values, values)


def shard_levels(stream_key, shape, pieces, smallest, top_value):
    gain = 1.0
    for position, parts in pieces:
        draws = jax.random.uniform(jax.random.fold_in(jax.random.fold_in(stream_key, 6), position), (parts,), jnp.float32, smallest / len(pieces), top_value / len(pieces))
        gain = gain * jnp.repeat(jnp.exp(draws), shape[position] // parts).reshape((-1,) + (1,) * (len(shape) - 1 - position))
    return gain


def bell_draw(own_key, extent, spread, limit, shards=(), kind=jnp.bfloat16):
    array = jax.random.normal(own_key, extent, jnp.float32) * spread
    if len(shards) > 0:
        array = shard_levels(own_key, extent, shards, -0.22, 0.18) * array
    return jnp.clip(array, min=-limit, max=limit).astype(kind)


def noise_with(stream_key, shape, scale, most, shards, heavy, kind=jnp.bfloat16):
    entries = scale * jax.random.normal(stream_key, shape, jnp.float32)
    if shards:
        entries = entries * shard_levels(stream_key, shape, shards, -0.22, 0.18)
    return jnp.clip(with_spikes(entries, jax.random.fold_in(stream_key, 3), *heavy), -most, most).astype(kind)


def setup_inputs(seed: int = 0) -> dict:
    streams_of = jax.random.split(jax.random.key(seed), 6)
    features = bell_draw(streams_of[0], (HEIGHT, COLS, C), 1.0, 6.0, ((0, 16), (2, 32)))
    w_in = noise_with(streams_of[1], (C, M), C ** -0.5, 0.1875, ((1, 32),), (1, 0, 32, 2.75))
    w_group = bell_draw(streams_of[2], (3, 3, GW, M), (9 * GW) ** -0.5, 0.25, ((3, 32),))
    w_out = noise_with(streams_of[3], (M, C), M ** -0.5, 0.1875, ((1, 32),), (1, 0, 32, 2.75))
    cotangent = bell_draw(streams_of[4], (HEIGHT, COLS, C), 1.0, 6.0, ((0, 16), (2, 32)))
    return {"features": features, "w_in": w_in, "w_group": w_group, "w_out": w_out, "cotangent": cotangent}


def silu_slope(values):
    sigma = jax.nn.sigmoid(values)
    return sigma * (1.0 + values * (1.0 - sigma))


def round_keep(values):
    rounded = lax.optimization_barrier(values.astype(jnp.bfloat16))
    return rounded.astype(jnp.float32)


def block_partials(left, right, blocks):
    pixel_count = left.shape[0]
    other_count = right.shape[0]
    left_blocks = left.reshape(pixel_count, blocks, -1).transpose(1, 0, 2)
    right_blocks = right.reshape(other_count, blocks, -1).transpose(1, 0, 2)

    def add_block(total, pair):
        piece = jnp.dot(pair[0], pair[1].T, preferred_element_type=jnp.float32)
        return total + round_keep(piece), None

    start_total = jnp.zeros((pixel_count, other_count), jnp.float32)
    total, unused = lax.scan(add_block, start_total, (left_blocks, right_blocks))
    return total


def group_forward(padded, taps, height, breadth):
    total = jnp.zeros((height, breadth, padded.shape[2], padded.shape[3]), jnp.float32)
    for row_tap in range(3):
        for col_tap in range(3):
            window = padded[row_tap:row_tap + height, col_tap:col_tap + breadth]
            total = total + jnp.einsum("rcgi,igj->rcgj", window, taps[row_tap, col_tap])
    return total


def group_backward(padded, taps, height, breadth):
    total = jnp.zeros((height, breadth, padded.shape[2], padded.shape[3]), jnp.float32)
    for row_tap in range(3):
        for col_tap in range(3):
            window = padded[2 - row_tap:2 - row_tap + height, 2 - col_tap:2 - col_tap + breadth]
            total = total + jnp.einsum("rcgj,igj->rcgi", window, taps[row_tap, col_tap])
    return total


def group_weight(padded, grads, height, breadth):
    rows_of_taps = []
    for row_tap in range(3):
        line = []
        for col_tap in range(3):
            window = padded[row_tap:row_tap + height, col_tap:col_tap + breadth]
            line.append(jnp.einsum("rcgi,rcgj->igj", window, grads))
        rows_of_taps.append(jnp.stack(line))
    return jnp.stack(rows_of_taps)


def reference(features, w_in, w_group, w_out, cotangent):
    height = ROW_DEV * N_ROW
    breadth = COLS
    pixel_count = height * breadth
    flat_in = features.reshape(pixel_count, C)
    pre_one = jnp.dot(flat_in, w_in, preferred_element_type=jnp.float32)
    act_one = jax.nn.silu(pre_one).astype(jnp.bfloat16)
    taps = w_group.astype(jnp.float32).reshape(3, 3, GW, GROUPS, GW)
    edge = ((1, 1), (1, 1), (0, 0), (0, 0))
    padded_one = jnp.pad(act_one.reshape(height, breadth, GROUPS, GW).astype(jnp.float32), edge)
    pre_two = group_forward(padded_one, taps, height, breadth).reshape(pixel_count, M)
    act_two = jax.nn.silu(pre_two).astype(jnp.bfloat16)
    branch = jnp.dot(act_two, w_out, preferred_element_type=jnp.float32)
    block_out = (flat_in.astype(jnp.float32) + branch).astype(jnp.bfloat16).reshape(height, breadth, C)
    grad_flat = cotangent.reshape(pixel_count, C)
    d_two = block_partials(grad_flat, w_out, N_CH)
    grad_two = (d_two * silu_slope(pre_two)).astype(jnp.bfloat16)
    padded_two = jnp.pad(grad_two.reshape(height, breadth, GROUPS, GW).astype(jnp.float32), edge)
    d_one = group_backward(padded_two, taps, height, breadth).reshape(pixel_count, M)
    grad_one = (d_one * silu_slope(pre_one)).astype(jnp.bfloat16)
    d_input = block_partials(grad_one, w_in, N_CH)
    grad_input = (grad_flat.astype(jnp.float32) + d_input).astype(jnp.bfloat16).reshape(height, breadth, C)
    band = ROW_DEV * breadth

    def add_band(totals, index):
        first = (index * band).astype(jnp.int32)
        in_band = lax.dynamic_slice_in_dim(flat_in, first, band, 0)
        one_band = lax.dynamic_slice_in_dim(grad_one, first, band, 0)
        mid_band = lax.dynamic_slice_in_dim(act_two, first, band, 0)
        cot_band = lax.dynamic_slice_in_dim(grad_flat, first, band, 0)
        in_part = jnp.dot(in_band.T, one_band, preferred_element_type=jnp.float32)
        out_part = jnp.dot(mid_band.T, cot_band, preferred_element_type=jnp.float32)
        top_row = (index * ROW_DEV).astype(jnp.int32)
        pad_band = lax.dynamic_slice_in_dim(padded_one, top_row, ROW_DEV + 2, 0)
        two_band = lax.dynamic_slice_in_dim(grad_two, first, band, 0)
        two_band = two_band.reshape(ROW_DEV, breadth, GROUPS, GW).astype(jnp.float32)
        group_part = group_weight(pad_band, two_band, ROW_DEV, breadth).reshape(3, 3, GW, M)
        return (totals[0] + round_keep(in_part), totals[1] + round_keep(out_part), totals[2] + round_keep(group_part)), None

    start_totals = (jnp.zeros((C, M), jnp.float32), jnp.zeros((M, C), jnp.float32), jnp.zeros((3, 3, GW, M), jnp.float32))
    totals, unused = lax.scan(add_band, start_totals, jnp.arange(N_ROW, dtype=jnp.int32))
    return (block_out, grad_input, totals[0].astype(jnp.bfloat16), totals[2].astype(jnp.bfloat16), totals[1].astype(jnp.bfloat16))
```

```python
import jax
import jax.numpy as jnp
from jax import lax
from jax.sharding import PartitionSpec as P


def padded_2(cells, sides, width):
    for axis, dim in sides:
        count = lax.axis_size(axis)
        ends = count - 1
        head = lax.slice_in_dim(cells, 0, width, axis=dim)
        tail = lax.slice_in_dim(cells, cells.shape[dim] - width, cells.shape[dim], axis=dim)
        cells = jnp.concatenate(
            [
                lax.ppermute(tail, axis, [(i, (i + 1) % count) for i in range(ends)]),
                cells,
                lax.ppermute(head, axis, [((i + 1) % count, i) for i in range(ends)]),
            ],
            axis=dim,
        )
    return cells


def silu_slope(values):
    sigma = jax.nn.sigmoid(values)
    return sigma * (1.0 + values * (1.0 - sigma))


def gather_blocks(local, axis):
    count = lax.axis_size(axis)
    spread = jnp.broadcast_to(local[None], (count,) + local.shape)
    return lax.all_to_all(spread, axis, 0, 0, tiled=True)


def sum_blocks(parts, axis):
    got = lax.all_to_all(parts, axis, 0, 0, tiled=True)
    return jnp.sum(got.astype(jnp.float32), axis=0)


def row_rims(local):
    padded = padded_2(local, (("row", 0),), 1)
    return jnp.pad(padded, ((0, 0), (1, 1), (0, 0)))


def group_view(local, group_width):
    return local.reshape(local.shape[0], local.shape[1], local.shape[2] // group_width, group_width)


def body(features, w_in, w_group, w_out, cotangent):
    row_count, col_count, local_ch = features.shape
    group_width = w_group.shape[2]
    local_mid = w_in.shape[1]
    pixel_count = row_count * col_count
    blocks = lax.axis_size("ch")
    bands = lax.axis_size("row")
    flat_local = features.reshape(pixel_count, local_ch)
    grad_flat = cotangent.reshape(pixel_count, local_ch)
    w_in_blocks = w_in.reshape(blocks, -1, local_mid)
    w_out_blocks = w_out.reshape(blocks, -1, local_ch)

    gathered = gather_blocks(flat_local, "ch")
    pre_one = jnp.einsum("jpc,jcm->pm", gathered, w_in_blocks, preferred_element_type=jnp.float32)
    act_one = jax.nn.silu(pre_one).astype(jnp.bfloat16).reshape(row_count, col_count, local_mid)
    padded_one = group_view(row_rims(act_one), group_width)
    filters = w_group.reshape(3, 3, group_width, local_mid // group_width, group_width)
    pre_two = jnp.zeros((row_count, col_count, local_mid // group_width, group_width), jnp.float32)
    for row_tap in range(3):
        for col_tap in range(3):
            window = padded_one[row_tap : row_tap + row_count, col_tap : col_tap + col_count]
            pre_two = pre_two + jnp.einsum(
                "rcgi,igj->rcgj",
                window,
                filters[row_tap, col_tap],
                preferred_element_type=jnp.float32,
            )
    pre_two = pre_two.reshape(pixel_count, local_mid)
    act_two = jax.nn.silu(pre_two).astype(jnp.bfloat16)
    mid_full = gather_blocks(act_two, "ch")
    branch = jnp.einsum("jpm,jmc->pc", mid_full, w_out_blocks, preferred_element_type=jnp.float32)
    block_out = (
        (flat_local.astype(jnp.float32) + branch)
        .astype(jnp.bfloat16)
        .reshape(row_count, col_count, local_ch)
    )
    two_parts = jnp.einsum(
        "pc,jmc->jpm", grad_flat, w_out_blocks, preferred_element_type=jnp.float32
    ).astype(jnp.bfloat16)
    d_two = sum_blocks(two_parts, "ch")
    grad_two = (d_two * silu_slope(pre_two)).astype(jnp.bfloat16)
    padded_two = group_view(
        row_rims(grad_two.reshape(row_count, col_count, local_mid)), group_width
    )
    d_one = jnp.zeros((row_count, col_count, local_mid // group_width, group_width), jnp.float32)
    for row_tap in range(3):
        for col_tap in range(3):
            window = padded_two[
                2 - row_tap : 2 - row_tap + row_count, 2 - col_tap : 2 - col_tap + col_count
            ]
            d_one = d_one + jnp.einsum(
                "rcgj,igj->rcgi",
                window,
                filters[row_tap, col_tap],
                preferred_element_type=jnp.float32,
            )
    grad_one = (d_one.reshape(pixel_count, local_mid) * silu_slope(pre_one)).astype(jnp.bfloat16)
    grad_view = group_view(grad_two.reshape(row_count, col_count, local_mid), group_width)
    tap_rows = []
    for row_tap in range(3):
        tap_line = []
        for col_tap in range(3):
            window = padded_one[row_tap : row_tap + row_count, col_tap : col_tap + col_count]
            tap_line.append(
                jnp.einsum("rcgi,rcgj->igj", window, grad_view, preferred_element_type=jnp.float32)
            )
        tap_rows.append(jnp.stack(tap_line))
    group_grad = jnp.stack(tap_rows).reshape(3, 3, group_width, local_mid)
    in_grad = jnp.einsum("jpc,pm->jcm", gathered, grad_one, preferred_element_type=jnp.float32)
    out_grad = jnp.einsum("jpm,pc->jmc", mid_full, grad_flat, preferred_element_type=jnp.float32)
    one_parts = jnp.einsum(
        "pm,jcm->jpc", grad_one, w_in_blocks, preferred_element_type=jnp.float32
    ).astype(jnp.bfloat16)
    d_input = sum_blocks(one_parts, "ch")
    grad_input = (
        (grad_flat.astype(jnp.float32) + d_input)
        .astype(jnp.bfloat16)
        .reshape(row_count, col_count, local_ch)
    )
    pieces = (in_grad, out_grad, group_grad)
    sizes = [piece.size for piece in pieces]
    packed = jnp.concatenate([piece.astype(jnp.bfloat16).reshape(-1) for piece in pieces])
    share = packed.size // bands
    reduced = sum_blocks(packed.reshape(bands, share), "row").astype(jnp.bfloat16)
    whole = gather_blocks(reduced, "row").reshape(-1)
    outs = []
    start = 0
    for piece, size in zip(pieces, sizes):
        outs.append(whole[start : start + size].reshape(piece.shape))
        start += size
    return (
        block_out,
        grad_input,
        outs[0].reshape(-1, local_mid),
        outs[2],
        outs[1].reshape(-1, local_ch),
    )


def solution(mesh):
    placed = (
        P("row", None, "ch"),
        P(None, "ch"),
        P(None, None, None, "ch"),
        P(None, "ch"),
        P("row", None, "ch"),
    )
    return jax.shard_map(
        body,
        mesh=mesh,
        in_specs=placed,
        out_specs=(
            P("row", None, "ch"),
            P("row", None, "ch"),
            P(None, "ch"),
            P(None, None, None, "ch"),
            P(None, "ch"),
        ),
        check_vma=False,
    )
```

```python
import jax
import jax.numpy as jnp
from jax import lax
from jax.sharding import Mesh, PartitionSpec as P


def padded_2(cells, sides, width):
    for axis, dim in sides:
        count = lax.axis_size(axis)
        ends = count - 1
        head = lax.slice_in_dim(cells, 0, width, axis=dim)
        tail = lax.slice_in_dim(cells, cells.shape[dim] - width, cells.shape[dim], axis=dim)
        cells = jnp.concatenate(
            [
                lax.ppermute(tail, axis, [(i, (i + 1) % count) for i in range(ends)]),
                cells,
                lax.ppermute(head, axis, [((i + 1) % count, i) for i in range(ends)]),
            ],
            axis=dim,
        )
    return cells


def silu_slope(values):
    sigma = jax.nn.sigmoid(values)
    return sigma * (1.0 + values * (1.0 - sigma))


def swap_core(value):
    return lax.ppermute(value, "core", [(0, 1), (1, 0)])


def gather_ch(local):
    along_z = lax.all_gather(local, "z", axis=0, tiled=False)
    mine = lax.axis_index("core")
    other = swap_core(along_z)
    return jnp.stack([jnp.where(mine == 0, along_z, other), jnp.where(mine == 0, other, along_z)])


def scatter_ch(parts):
    mine = lax.axis_index("core")
    keep = jnp.where(mine == 0, parts[:, 0], parts[:, 1])
    send = jnp.where(mine == 0, parts[:, 1], parts[:, 0])
    on_chip = (keep.astype(jnp.float32) + swap_core(send).astype(jnp.float32)).astype(jnp.bfloat16)
    return lax.psum_scatter(on_chip, "z", scatter_dimension=0, tiled=True)[0]


def row_rims(local):
    padded = padded_2(local, (("row", 0),), 1)
    return jnp.pad(padded, ((0, 0), (1, 1), (0, 0)))


def group_view(local, group_width):
    return local.reshape(local.shape[0], local.shape[1], local.shape[2] // group_width, group_width)


def body(features, w_in, w_group, w_out, cotangent):
    row_count, col_count, local_ch = features.shape
    group_width = w_group.shape[2]
    local_mid = w_in.shape[1]
    pixel_count = row_count * col_count
    chips = lax.axis_size("z")
    cores = lax.axis_size("core")
    flat_local = features.reshape(pixel_count, local_ch)
    grad_flat = cotangent.reshape(pixel_count, local_ch)
    w_in_blocks = w_in.reshape(chips, cores, -1, local_mid)
    w_out_blocks = w_out.reshape(chips, cores, -1, local_ch)

    gathered = gather_ch(flat_local)
    pre_one = jnp.einsum("kzpc,zkcm->pm", gathered, w_in_blocks, preferred_element_type=jnp.float32)
    act_one = jax.nn.silu(pre_one).astype(jnp.bfloat16).reshape(row_count, col_count, local_mid)
    padded_one = group_view(row_rims(act_one), group_width)
    filters = w_group.reshape(3, 3, group_width, local_mid // group_width, group_width)
    pre_two = jnp.zeros((row_count, col_count, local_mid // group_width, group_width), jnp.float32)
    for row_tap in range(3):
        for col_tap in range(3):
            window = padded_one[row_tap : row_tap + row_count, col_tap : col_tap + col_count]
            pre_two = pre_two + jnp.einsum(
                "rcgi,igj->rcgj",
                window,
                filters[row_tap, col_tap],
                preferred_element_type=jnp.float32,
            )
    pre_two = pre_two.reshape(pixel_count, local_mid)
    act_two = jax.nn.silu(pre_two).astype(jnp.bfloat16)
    mid_full = gather_ch(act_two)
    branch = jnp.einsum("kzpm,zkmc->pc", mid_full, w_out_blocks, preferred_element_type=jnp.float32)
    block_out = (
        (flat_local.astype(jnp.float32) + branch)
        .astype(jnp.bfloat16)
        .reshape(row_count, col_count, local_ch)
    )
    two_parts = jnp.einsum(
        "pc,zkmc->zkpm", grad_flat, w_out_blocks, preferred_element_type=jnp.float32
    ).astype(jnp.bfloat16)
    d_two = scatter_ch(two_parts).astype(jnp.float32)
    grad_two = (d_two * silu_slope(pre_two)).astype(jnp.bfloat16)
    padded_two = group_view(
        row_rims(grad_two.reshape(row_count, col_count, local_mid)), group_width
    )
    d_one = jnp.zeros((row_count, col_count, local_mid // group_width, group_width), jnp.float32)
    for row_tap in range(3):
        for col_tap in range(3):
            window = padded_two[
                2 - row_tap : 2 - row_tap + row_count, 2 - col_tap : 2 - col_tap + col_count
            ]
            d_one = d_one + jnp.einsum(
                "rcgj,igj->rcgi",
                window,
                filters[row_tap, col_tap],
                preferred_element_type=jnp.float32,
            )
    grad_one = (d_one.reshape(pixel_count, local_mid) * silu_slope(pre_one)).astype(jnp.bfloat16)
    grad_view = group_view(grad_two.reshape(row_count, col_count, local_mid), group_width)
    tap_rows = []
    for row_tap in range(3):
        tap_line = []
        for col_tap in range(3):
            window = padded_one[row_tap : row_tap + row_count, col_tap : col_tap + col_count]
            tap_line.append(
                jnp.einsum("rcgi,rcgj->igj", window, grad_view, preferred_element_type=jnp.float32)
            )
        tap_rows.append(jnp.stack(tap_line))
    group_grad = jnp.stack(tap_rows).reshape(3, 3, group_width, local_mid)
    in_grad = jnp.einsum("kzpc,pm->zkcm", gathered, grad_one, preferred_element_type=jnp.float32)
    out_grad = jnp.einsum("kzpm,pc->zkmc", mid_full, grad_flat, preferred_element_type=jnp.float32)
    one_parts = jnp.einsum(
        "pm,zkcm->zkpc", grad_one, w_in_blocks, preferred_element_type=jnp.float32
    ).astype(jnp.bfloat16)
    d_input = scatter_ch(one_parts).astype(jnp.float32)
    grad_input = (
        (grad_flat.astype(jnp.float32) + d_input)
        .astype(jnp.bfloat16)
        .reshape(row_count, col_count, local_ch)
    )
    outs = (
        lax.psum(in_grad.astype(jnp.bfloat16), "row"),
        lax.psum(out_grad.astype(jnp.bfloat16), "row"),
        lax.psum(group_grad.astype(jnp.bfloat16), "row"),
    )
    return (
        block_out,
        grad_input,
        outs[0].reshape(-1, local_mid),
        outs[2],
        outs[1].reshape(-1, local_ch),
    )


def solution(mesh):
    rows, channels = mesh.devices.shape
    fine = Mesh(mesh.devices.reshape(rows, channels // 2, 2), ("row", "z", "core"))
    ch = ("z", "core")
    placed = (
        P("row", None, ch),
        P(None, ch),
        P(None, None, None, ch),
        P(None, ch),
        P("row", None, ch),
    )
    return jax.shard_map(
        body,
        mesh=fine,
        in_specs=placed,
        out_specs=(
            P("row", None, ch),
            P("row", None, ch),
            P(None, ch),
            P(None, None, None, ch),
            P(None, ch),
        ),
        check_vma=False,
    )
```

```python
import jax
import jax.numpy as jnp
from jax import lax
from jax.sharding import Mesh, PartitionSpec as P


def padded_2(cells, sides, width):
    for axis, dim in sides:
        count = lax.axis_size(axis)
        ends = count - 1
        head = lax.slice_in_dim(cells, 0, width, axis=dim)
        tail = lax.slice_in_dim(cells, cells.shape[dim] - width, cells.shape[dim], axis=dim)
        cells = jnp.concatenate(
            [
                lax.ppermute(tail, axis, [(i, (i + 1) % count) for i in range(ends)]),
                cells,
                lax.ppermute(head, axis, [((i + 1) % count, i) for i in range(ends)]),
            ],
            axis=dim,
        )
    return cells


def silu_slope(values):
    sigma = jax.nn.sigmoid(values)
    return sigma * (1.0 + values * (1.0 - sigma))


def swap_core(value):
    return lax.ppermute(value, "core", [(0, 1), (1, 0)])


def ring_gather(local, axis):
    count = lax.axis_size(axis)
    me = lax.axis_index(axis)
    ahead = [(i, (i + 1) % count) for i in range(count)]
    behind = [(i, (i - 1) % count) for i in range(count)]
    by_offset = [local] + [None] * (count - 1)
    from_behind = local
    from_ahead = local
    for step in range(1, count // 2 + 1):
        from_behind = lax.ppermute(from_behind, axis, ahead)
        by_offset[count - step] = from_behind
        if step < count - step:
            from_ahead = lax.ppermute(from_ahead, axis, behind)
            by_offset[step] = from_ahead
    stacked = jnp.stack(by_offset)
    doubled = jnp.concatenate([stacked, stacked])
    return lax.dynamic_slice_in_dim(doubled, count - me, count, 0)


def ring_scatter(parts, axis):
    count = lax.axis_size(axis)
    me = lax.axis_index(axis)
    ahead = [(i, (i + 1) % count) for i in range(count)]
    behind = [(i, (i - 1) % count) for i in range(count)]
    far_behind = count // 2
    far_ahead = count - 1 - far_behind

    def block(offset):
        return lax.dynamic_index_in_dim(parts, (me + offset) % count, 0, keepdims=False).astype(jnp.float32)

    total = block(0)
    carry = None
    for step in range(far_behind):
        mine = block(far_behind - step)
        carry = mine if carry is None else carry + mine
        carry = lax.ppermute(carry.astype(jnp.bfloat16), axis, ahead).astype(jnp.float32)
    total = total + carry
    carry = None
    for step in range(far_ahead):
        mine = block(step - far_ahead)
        carry = mine if carry is None else carry + mine
        carry = lax.ppermute(carry.astype(jnp.bfloat16), axis, behind).astype(jnp.float32)
    return total + carry


def gather_ch(local):
    along_z = ring_gather(local, "z")
    mine = lax.axis_index("core")
    other = swap_core(along_z)
    return jnp.stack([jnp.where(mine == 0, along_z, other), jnp.where(mine == 0, other, along_z)])


def scatter_ch(parts):
    mine = lax.axis_index("core")
    keep = jnp.where(mine == 0, parts[:, 0], parts[:, 1])
    send = jnp.where(mine == 0, parts[:, 1], parts[:, 0])
    on_chip = (keep.astype(jnp.float32) + swap_core(send).astype(jnp.float32)).astype(jnp.bfloat16)
    return ring_scatter(on_chip, "z")


def row_rims(local):
    padded = padded_2(local, (("row", 0),), 1)
    return jnp.pad(padded, ((0, 0), (1, 1), (0, 0)))


def group_view(local, group_width):
    return local.reshape(local.shape[0], local.shape[1], local.shape[2] // group_width, group_width)


def body(features, w_in, w_group, w_out, cotangent):
    row_count, col_count, local_ch = features.shape
    group_width = w_group.shape[2]
    local_mid = w_in.shape[1]
    pixel_count = row_count * col_count
    chips = lax.axis_size("z")
    cores = lax.axis_size("core")
    flat_local = features.reshape(pixel_count, local_ch)
    grad_flat = cotangent.reshape(pixel_count, local_ch)
    w_in_blocks = w_in.reshape(chips, cores, -1, local_mid)
    w_out_blocks = w_out.reshape(chips, cores, -1, local_ch)

    gathered = gather_ch(flat_local)
    pre_one = jnp.einsum("kzpc,zkcm->pm", gathered, w_in_blocks, preferred_element_type=jnp.float32)
    act_one = jax.nn.silu(pre_one).astype(jnp.bfloat16).reshape(row_count, col_count, local_mid)
    padded_one = group_view(row_rims(act_one), group_width)
    filters = w_group.reshape(3, 3, group_width, local_mid // group_width, group_width)
    pre_two = jnp.zeros((row_count, col_count, local_mid // group_width, group_width), jnp.float32)
    for row_tap in range(3):
        for col_tap in range(3):
            window = padded_one[row_tap : row_tap + row_count, col_tap : col_tap + col_count]
            pre_two = pre_two + jnp.einsum(
                "rcgi,igj->rcgj",
                window,
                filters[row_tap, col_tap],
                preferred_element_type=jnp.float32,
            )
    pre_two = pre_two.reshape(pixel_count, local_mid)
    act_two = jax.nn.silu(pre_two).astype(jnp.bfloat16)
    mid_full = gather_ch(act_two)
    branch = jnp.einsum("kzpm,zkmc->pc", mid_full, w_out_blocks, preferred_element_type=jnp.float32)
    block_out = (
        (flat_local.astype(jnp.float32) + branch)
        .astype(jnp.bfloat16)
        .reshape(row_count, col_count, local_ch)
    )
    two_parts = jnp.einsum(
        "pc,zkmc->zkpm", grad_flat, w_out_blocks, preferred_element_type=jnp.float32
    ).astype(jnp.bfloat16)
    d_two = scatter_ch(two_parts)
    grad_two = (d_two * silu_slope(pre_two)).astype(jnp.bfloat16)
    padded_two = group_view(
        row_rims(grad_two.reshape(row_count, col_count, local_mid)), group_width
    )
    d_one = jnp.zeros((row_count, col_count, local_mid // group_width, group_width), jnp.float32)
    for row_tap in range(3):
        for col_tap in range(3):
            window = padded_two[
                2 - row_tap : 2 - row_tap + row_count, 2 - col_tap : 2 - col_tap + col_count
            ]
            d_one = d_one + jnp.einsum(
                "rcgj,igj->rcgi",
                window,
                filters[row_tap, col_tap],
                preferred_element_type=jnp.float32,
            )
    grad_one = (d_one.reshape(pixel_count, local_mid) * silu_slope(pre_one)).astype(jnp.bfloat16)
    grad_view = group_view(grad_two.reshape(row_count, col_count, local_mid), group_width)
    tap_rows = []
    for row_tap in range(3):
        tap_line = []
        for col_tap in range(3):
            window = padded_one[row_tap : row_tap + row_count, col_tap : col_tap + col_count]
            tap_line.append(
                jnp.einsum("rcgi,rcgj->igj", window, grad_view, preferred_element_type=jnp.float32)
            )
        tap_rows.append(jnp.stack(tap_line))
    group_grad = jnp.stack(tap_rows).reshape(3, 3, group_width, local_mid)
    in_grad = jnp.einsum("kzpc,pm->zkcm", gathered, grad_one, preferred_element_type=jnp.float32)
    out_grad = jnp.einsum("kzpm,pc->zkmc", mid_full, grad_flat, preferred_element_type=jnp.float32)
    one_parts = jnp.einsum(
        "pm,zkcm->zkpc", grad_one, w_in_blocks, preferred_element_type=jnp.float32
    ).astype(jnp.bfloat16)
    d_input = scatter_ch(one_parts)
    grad_input = (
        (grad_flat.astype(jnp.float32) + d_input)
        .astype(jnp.bfloat16)
        .reshape(row_count, col_count, local_ch)
    )
    outs = (
        lax.psum(in_grad.astype(jnp.bfloat16), "row"),
        lax.psum(out_grad.astype(jnp.bfloat16), "row"),
        lax.psum(group_grad.astype(jnp.bfloat16), "row"),
    )
    return (
        block_out,
        grad_input,
        outs[0].reshape(-1, local_mid),
        outs[2],
        outs[1].reshape(-1, local_ch),
    )


def solution(mesh):
    rows, channels = mesh.devices.shape
    fine = Mesh(mesh.devices.reshape(rows, channels // 2, 2), ("row", "z", "core"))
    ch = ("z", "core")
    placed = (
        P("row", None, ch),
        P(None, ch),
        P(None, None, None, ch),
        P(None, ch),
        P("row", None, ch),
    )
    return jax.shard_map(
        body,
        mesh=fine,
        in_specs=placed,
        out_specs=(
            P("row", None, ch),
            P("row", None, ch),
            P(None, ch),
            P(None, None, None, ch),
            P(None, ch),
        ),
        check_vma=False,
    )
```

```python
import jax
import jax.numpy as jnp
from jax import lax
from jax.sharding import Mesh, PartitionSpec as P


def padded_2(cells, sides, width):
    for axis, dim in sides:
        count = lax.axis_size(axis)
        ends = count - 1
        head = lax.slice_in_dim(cells, 0, width, axis=dim)
        tail = lax.slice_in_dim(cells, cells.shape[dim] - width, cells.shape[dim], axis=dim)
        cells = jnp.concatenate(
            [
                lax.ppermute(tail, axis, [(i, (i + 1) % count) for i in range(ends)]),
                cells,
                lax.ppermute(head, axis, [((i + 1) % count, i) for i in range(ends)]),
            ],
            axis=dim,
        )
    return cells


def silu_slope(values):
    sigma = jax.nn.sigmoid(values)
    return sigma * (1.0 + values * (1.0 - sigma))


def swap_core(value):
    return lax.ppermute(value, "core", [(0, 1), (1, 0)])


def ring_gather(local, axis):
    count = lax.axis_size(axis)
    me = lax.axis_index(axis)
    ahead = [(i, (i + 1) % count) for i in range(count)]
    behind = [(i, (i - 1) % count) for i in range(count)]
    by_offset = [local] + [None] * (count - 1)
    from_behind = local
    from_ahead = local
    for step in range(1, count // 2 + 1):
        from_behind = lax.ppermute(from_behind, axis, ahead)
        by_offset[count - step] = from_behind
        if step < count - step:
            from_ahead = lax.ppermute(from_ahead, axis, behind)
            by_offset[step] = from_ahead
    stacked = jnp.stack(by_offset)
    doubled = jnp.concatenate([stacked, stacked])
    return lax.dynamic_slice_in_dim(doubled, count - me, count, 0)


def ring_scatter(parts, axis):
    count = lax.axis_size(axis)
    me = lax.axis_index(axis)
    ahead = [(i, (i + 1) % count) for i in range(count)]
    behind = [(i, (i - 1) % count) for i in range(count)]
    far_behind = count // 2
    far_ahead = count - 1 - far_behind

    def block(offset):
        return lax.dynamic_index_in_dim(parts, (me + offset) % count, 0, keepdims=False).astype(jnp.float32)

    total = block(0)
    carry = None
    for step in range(far_behind):
        mine = block(far_behind - step)
        carry = mine if carry is None else carry + mine
        carry = lax.ppermute(carry.astype(jnp.bfloat16), axis, ahead).astype(jnp.float32)
    total = total + carry
    carry = None
    for step in range(far_ahead):
        mine = block(step - far_ahead)
        carry = mine if carry is None else carry + mine
        carry = lax.ppermute(carry.astype(jnp.bfloat16), axis, behind).astype(jnp.float32)
    return total + carry


def add_up(stack):
    total = stack[0].astype(jnp.float32)
    for index in range(1, stack.shape[0]):
        total = total + stack[index].astype(jnp.float32)
    return total


def gather_ch(local):
    along_z = lax.all_gather(local, "z", axis=0, tiled=False)
    mine = lax.axis_index("core")
    other = swap_core(along_z)
    return jnp.stack([jnp.where(mine == 0, along_z, other), jnp.where(mine == 0, other, along_z)])


def scatter_ch(parts):
    mine = lax.axis_index("core")
    keep = jnp.where(mine == 0, parts[:, 0], parts[:, 1])
    send = jnp.where(mine == 0, parts[:, 1], parts[:, 0])
    on_chip = (keep.astype(jnp.float32) + swap_core(send).astype(jnp.float32)).astype(jnp.bfloat16)
    return add_up(lax.all_to_all(on_chip, "z", 0, 0, tiled=True))


def sum_rows(pieces):
    bands = lax.axis_size("row")
    packed = jnp.concatenate([piece.astype(jnp.bfloat16).reshape(-1) for piece in pieces])
    share = packed.size // bands
    got = lax.all_to_all(packed.reshape(bands, share), "row", 0, 0, tiled=True)
    reduced = add_up(got).astype(jnp.bfloat16)
    spread = jnp.broadcast_to(reduced[None], (bands, share))
    whole = lax.all_to_all(spread, "row", 0, 0, tiled=True).reshape(-1)
    outs = []
    start = 0
    for piece in pieces:
        outs.append(whole[start : start + piece.size].reshape(piece.shape))
        start += piece.size
    return outs


def row_rims(local):
    padded = padded_2(local, (("row", 0),), 1)
    return jnp.pad(padded, ((0, 0), (1, 1), (0, 0)))


def group_view(local, group_width):
    return local.reshape(local.shape[0], local.shape[1], local.shape[2] // group_width, group_width)


def body(features, w_in, w_group, w_out, cotangent):
    row_count, col_count, local_ch = features.shape
    group_width = w_group.shape[2]
    local_mid = w_in.shape[1]
    pixel_count = row_count * col_count
    chips = lax.axis_size("z")
    cores = lax.axis_size("core")
    flat_local = features.reshape(pixel_count, local_ch)
    grad_flat = cotangent.reshape(pixel_count, local_ch)
    w_in_blocks = w_in.reshape(chips, cores, -1, local_mid)
    w_out_blocks = w_out.reshape(chips, cores, -1, local_ch)

    gathered = gather_ch(flat_local)
    pre_one = jnp.einsum("kzpc,zkcm->pm", gathered, w_in_blocks, preferred_element_type=jnp.float32)
    act_one = jax.nn.silu(pre_one).astype(jnp.bfloat16).reshape(row_count, col_count, local_mid)
    padded_one = group_view(row_rims(act_one), group_width)
    filters = w_group.reshape(3, 3, group_width, local_mid // group_width, group_width)
    pre_two = jnp.zeros((row_count, col_count, local_mid // group_width, group_width), jnp.float32)
    for row_tap in range(3):
        for col_tap in range(3):
            window = padded_one[row_tap : row_tap + row_count, col_tap : col_tap + col_count]
            pre_two = pre_two + jnp.einsum(
                "rcgi,igj->rcgj",
                window,
                filters[row_tap, col_tap],
                preferred_element_type=jnp.float32,
            )
    pre_two = pre_two.reshape(pixel_count, local_mid)
    act_two = jax.nn.silu(pre_two).astype(jnp.bfloat16)
    mid_full = gather_ch(act_two)
    branch = jnp.einsum("kzpm,zkmc->pc", mid_full, w_out_blocks, preferred_element_type=jnp.float32)
    block_out = (
        (flat_local.astype(jnp.float32) + branch)
        .astype(jnp.bfloat16)
        .reshape(row_count, col_count, local_ch)
    )
    two_parts = jnp.einsum(
        "pc,zkmc->zkpm", grad_flat, w_out_blocks, preferred_element_type=jnp.float32
    ).astype(jnp.bfloat16)
    d_two = scatter_ch(two_parts)
    grad_two = (d_two * silu_slope(pre_two)).astype(jnp.bfloat16)
    padded_two = group_view(
        row_rims(grad_two.reshape(row_count, col_count, local_mid)), group_width
    )
    d_one = jnp.zeros((row_count, col_count, local_mid // group_width, group_width), jnp.float32)
    for row_tap in range(3):
        for col_tap in range(3):
            window = padded_two[
                2 - row_tap : 2 - row_tap + row_count, 2 - col_tap : 2 - col_tap + col_count
            ]
            d_one = d_one + jnp.einsum(
                "rcgj,igj->rcgi",
                window,
                filters[row_tap, col_tap],
                preferred_element_type=jnp.float32,
            )
    grad_one = (d_one.reshape(pixel_count, local_mid) * silu_slope(pre_one)).astype(jnp.bfloat16)
    grad_view = group_view(grad_two.reshape(row_count, col_count, local_mid), group_width)
    tap_rows = []
    for row_tap in range(3):
        tap_line = []
        for col_tap in range(3):
            window = padded_one[row_tap : row_tap + row_count, col_tap : col_tap + col_count]
            tap_line.append(
                jnp.einsum("rcgi,rcgj->igj", window, grad_view, preferred_element_type=jnp.float32)
            )
        tap_rows.append(jnp.stack(tap_line))
    group_grad = jnp.stack(tap_rows).reshape(3, 3, group_width, local_mid)
    in_grad = jnp.einsum("kzpc,pm->zkcm", gathered, grad_one, preferred_element_type=jnp.float32)
    out_grad = jnp.einsum("kzpm,pc->zkmc", mid_full, grad_flat, preferred_element_type=jnp.float32)
    one_parts = jnp.einsum(
        "pm,zkcm->zkpc", grad_one, w_in_blocks, preferred_element_type=jnp.float32
    ).astype(jnp.bfloat16)
    d_input = scatter_ch(one_parts)
    grad_input = (
        (grad_flat.astype(jnp.float32) + d_input)
        .astype(jnp.bfloat16)
        .reshape(row_count, col_count, local_ch)
    )
    outs = sum_rows((in_grad, out_grad, group_grad))
    return (
        block_out,
        grad_input,
        outs[0].reshape(-1, local_mid),
        outs[2],
        outs[1].reshape(-1, local_ch),
    )


def solution(mesh):
    rows, channels = mesh.devices.shape
    fine = Mesh(mesh.devices.reshape(rows, channels // 2, 2), ("row", "z", "core"))
    ch = ("z", "core")
    placed = (
        P("row", None, ch),
        P(None, ch),
        P(None, None, None, ch),
        P(None, ch),
        P("row", None, ch),
    )
    return jax.shard_map(
        body,
        mesh=fine,
        in_specs=placed,
        out_specs=(
            P("row", None, ch),
            P("row", None, ch),
            P(None, ch),
            P(None, None, None, ch),
            P(None, ch),
        ),
        check_vma=False,
    )
```

```python
import jax
import jax.numpy as jnp
from jax import lax
from jax.sharding import Mesh, PartitionSpec as P


def padded_2(cells, sides, width):
    for axis, dim in sides:
        count = lax.axis_size(axis)
        ends = count - 1
        head = lax.slice_in_dim(cells, 0, width, axis=dim)
        tail = lax.slice_in_dim(cells, cells.shape[dim] - width, cells.shape[dim], axis=dim)
        cells = jnp.concatenate(
            [
                lax.ppermute(tail, axis, [(i, (i + 1) % count) for i in range(ends)]),
                cells,
                lax.ppermute(head, axis, [((i + 1) % count, i) for i in range(ends)]),
            ],
            axis=dim,
        )
    return cells


def silu_slope(values):
    sigma = jax.nn.sigmoid(values)
    return sigma * (1.0 + values * (1.0 - sigma))


def swap_core(value):
    return lax.ppermute(value, "core", [(0, 1), (1, 0)])


def ring_gather(local, axis):
    count = lax.axis_size(axis)
    me = lax.axis_index(axis)
    ahead = [(i, (i + 1) % count) for i in range(count)]
    behind = [(i, (i - 1) % count) for i in range(count)]
    by_offset = [local] + [None] * (count - 1)
    from_behind = local
    from_ahead = local
    for step in range(1, count // 2 + 1):
        from_behind = lax.ppermute(from_behind, axis, ahead)
        by_offset[count - step] = from_behind
        if step < count - step:
            from_ahead = lax.ppermute(from_ahead, axis, behind)
            by_offset[step] = from_ahead
    stacked = jnp.stack(by_offset)
    doubled = jnp.concatenate([stacked, stacked])
    return lax.dynamic_slice_in_dim(doubled, count - me, count, 0)


def ring_scatter(parts, axis):
    count = lax.axis_size(axis)
    me = lax.axis_index(axis)
    ahead = [(i, (i + 1) % count) for i in range(count)]
    behind = [(i, (i - 1) % count) for i in range(count)]
    far_behind = count // 2
    far_ahead = count - 1 - far_behind

    def block(offset):
        return lax.dynamic_index_in_dim(parts, (me + offset) % count, 0, keepdims=False).astype(jnp.float32)

    total = block(0)
    carry = None
    for step in range(far_behind):
        mine = block(far_behind - step)
        carry = mine if carry is None else carry + mine
        carry = lax.ppermute(carry.astype(jnp.bfloat16), axis, ahead).astype(jnp.float32)
    total = total + carry
    carry = None
    for step in range(far_ahead):
        mine = block(step - far_ahead)
        carry = mine if carry is None else carry + mine
        carry = lax.ppermute(carry.astype(jnp.bfloat16), axis, behind).astype(jnp.float32)
    return total + carry


def add_up(stack):
    total = stack[0].astype(jnp.float32)
    for index in range(1, stack.shape[0]):
        total = total + stack[index].astype(jnp.float32)
    return total


def gather_ch(local):
    chips = lax.axis_size("z")
    along_z = lax.all_to_all(jnp.broadcast_to(local[None], (chips,) + local.shape), "z", 0, 0, tiled=True)
    mine = lax.axis_index("core")
    other = swap_core(along_z)
    return jnp.stack([jnp.where(mine == 0, along_z, other), jnp.where(mine == 0, other, along_z)])


def scatter_ch(parts):
    mine = lax.axis_index("core")
    keep = jnp.where(mine == 0, parts[:, 0], parts[:, 1])
    send = jnp.where(mine == 0, parts[:, 1], parts[:, 0])
    on_chip = (keep.astype(jnp.float32) + swap_core(send).astype(jnp.float32)).astype(jnp.bfloat16)
    return add_up(lax.all_to_all(on_chip, "z", 0, 0, tiled=True))


def sum_rows(pieces):
    bands = lax.axis_size("row")
    lanes = pieces[0].shape[-1]
    flat = [piece.astype(jnp.bfloat16).reshape(-1, lanes) for piece in pieces]
    rows = sum(part.shape[0] for part in flat)
    unit = bands * 16
    padded_rows = (rows + unit - 1) // unit * unit
    flat.append(jnp.zeros((padded_rows - rows, lanes), jnp.bfloat16))
    packed = jnp.concatenate(flat).reshape(bands, padded_rows // bands, lanes)
    got = lax.all_to_all(packed, "row", 0, 0, tiled=True)
    reduced = add_up(got).astype(jnp.bfloat16)
    spread = jnp.broadcast_to(reduced[None], packed.shape)
    whole = lax.all_to_all(spread, "row", 0, 0, tiled=True).reshape(padded_rows, lanes)
    outs = []
    start = 0
    for piece in pieces:
        size = piece.size // lanes
        outs.append(whole[start : start + size].reshape(piece.shape))
        start += size
    return outs


def row_rims(local):
    padded = padded_2(local, (("row", 0),), 1)
    return jnp.pad(padded, ((0, 0), (1, 1), (0, 0)))


def group_view(local, group_width):
    return local.reshape(local.shape[0], local.shape[1], local.shape[2] // group_width, group_width)


def body(features, w_in, w_group, w_out, cotangent):
    row_count, col_count, local_ch = features.shape
    group_width = w_group.shape[2]
    local_mid = w_in.shape[1]
    pixel_count = row_count * col_count
    chips = lax.axis_size("z")
    cores = lax.axis_size("core")
    flat_local = features.reshape(pixel_count, local_ch)
    grad_flat = cotangent.reshape(pixel_count, local_ch)
    w_in_blocks = w_in.reshape(chips, cores, -1, local_mid)
    w_out_blocks = w_out.reshape(chips, cores, -1, local_ch)

    gathered = gather_ch(flat_local)
    pre_one = jnp.einsum("kzpc,zkcm->pm", gathered, w_in_blocks, preferred_element_type=jnp.float32)
    act_one = jax.nn.silu(pre_one).astype(jnp.bfloat16).reshape(row_count, col_count, local_mid)
    padded_one = group_view(row_rims(act_one), group_width)
    filters = w_group.reshape(3, 3, group_width, local_mid // group_width, group_width)
    pre_two = jnp.zeros((row_count, col_count, local_mid // group_width, group_width), jnp.float32)
    for row_tap in range(3):
        for col_tap in range(3):
            window = padded_one[row_tap : row_tap + row_count, col_tap : col_tap + col_count]
            pre_two = pre_two + jnp.einsum(
                "rcgi,igj->rcgj",
                window,
                filters[row_tap, col_tap],
                preferred_element_type=jnp.float32,
            )
    pre_two = pre_two.reshape(pixel_count, local_mid)
    act_two = jax.nn.silu(pre_two).astype(jnp.bfloat16)
    mid_full = gather_ch(act_two)
    branch = jnp.einsum("kzpm,zkmc->pc", mid_full, w_out_blocks, preferred_element_type=jnp.float32)
    block_out = (
        (flat_local.astype(jnp.float32) + branch)
        .astype(jnp.bfloat16)
        .reshape(row_count, col_count, local_ch)
    )
    two_parts = jnp.einsum(
        "pc,zkmc->zkpm", grad_flat, w_out_blocks, preferred_element_type=jnp.float32
    ).astype(jnp.bfloat16)
    d_two = scatter_ch(two_parts)
    grad_two = (d_two * silu_slope(pre_two)).astype(jnp.bfloat16)
    padded_two = group_view(
        row_rims(grad_two.reshape(row_count, col_count, local_mid)), group_width
    )
    d_one = jnp.zeros((row_count, col_count, local_mid // group_width, group_width), jnp.float32)
    for row_tap in range(3):
        for col_tap in range(3):
            window = padded_two[
                2 - row_tap : 2 - row_tap + row_count, 2 - col_tap : 2 - col_tap + col_count
            ]
            d_one = d_one + jnp.einsum(
                "rcgj,igj->rcgi",
                window,
                filters[row_tap, col_tap],
                preferred_element_type=jnp.float32,
            )
    grad_one = (d_one.reshape(pixel_count, local_mid) * silu_slope(pre_one)).astype(jnp.bfloat16)
    grad_view = group_view(grad_two.reshape(row_count, col_count, local_mid), group_width)
    tap_rows = []
    for row_tap in range(3):
        tap_line = []
        for col_tap in range(3):
            window = padded_one[row_tap : row_tap + row_count, col_tap : col_tap + col_count]
            tap_line.append(
                jnp.einsum("rcgi,rcgj->igj", window, grad_view, preferred_element_type=jnp.float32)
            )
        tap_rows.append(jnp.stack(tap_line))
    group_grad = jnp.stack(tap_rows).reshape(3, 3, group_width, local_mid)
    in_grad = jnp.einsum("kzpc,pm->zkcm", gathered, grad_one, preferred_element_type=jnp.float32)
    out_grad = jnp.einsum("kzpm,pc->zkmc", mid_full, grad_flat, preferred_element_type=jnp.float32)
    one_parts = jnp.einsum(
        "pm,zkcm->zkpc", grad_one, w_in_blocks, preferred_element_type=jnp.float32
    ).astype(jnp.bfloat16)
    d_input = scatter_ch(one_parts)
    grad_input = (
        (grad_flat.astype(jnp.float32) + d_input)
        .astype(jnp.bfloat16)
        .reshape(row_count, col_count, local_ch)
    )
    outs = sum_rows((in_grad, out_grad, group_grad))
    return (
        block_out,
        grad_input,
        outs[0].reshape(-1, local_mid),
        outs[2],
        outs[1].reshape(-1, local_ch),
    )


def solution(mesh):
    rows, channels = mesh.devices.shape
    fine = Mesh(mesh.devices.reshape(rows, channels // 2, 2), ("row", "z", "core"))
    ch = ("z", "core")
    placed = (
        P("row", None, ch),
        P(None, ch),
        P(None, None, None, ch),
        P(None, ch),
        P("row", None, ch),
    )
    return jax.shard_map(
        body,
        mesh=fine,
        in_specs=placed,
        out_specs=(
            P("row", None, ch),
            P("row", None, ch),
            P(None, ch),
            P(None, None, None, ch),
            P(None, ch),
        ),
        check_vma=False,
    )
```

```python
import jax
import jax.numpy as jnp
from jax import lax
from jax.sharding import Mesh, PartitionSpec as P


def padded_2(cells, sides, width):
    for axis, dim in sides:
        count = lax.axis_size(axis)
        ends = count - 1
        head = lax.slice_in_dim(cells, 0, width, axis=dim)
        tail = lax.slice_in_dim(cells, cells.shape[dim] - width, cells.shape[dim], axis=dim)
        cells = jnp.concatenate(
            [
                lax.ppermute(tail, axis, [(i, (i + 1) % count) for i in range(ends)]),
                cells,
                lax.ppermute(head, axis, [((i + 1) % count, i) for i in range(ends)]),
            ],
            axis=dim,
        )
    return cells


def silu_slope(values):
    sigma = jax.nn.sigmoid(values)
    return sigma * (1.0 + values * (1.0 - sigma))


def swap_core(value):
    return lax.ppermute(value, "core", [(0, 1), (1, 0)])


def ring_gather(local, axis):
    count = lax.axis_size(axis)
    me = lax.axis_index(axis)
    ahead = [(i, (i + 1) % count) for i in range(count)]
    behind = [(i, (i - 1) % count) for i in range(count)]
    by_offset = [local] + [None] * (count - 1)
    from_behind = local
    from_ahead = local
    for step in range(1, count // 2 + 1):
        from_behind = lax.ppermute(from_behind, axis, ahead)
        by_offset[count - step] = from_behind
        if step < count - step:
            from_ahead = lax.ppermute(from_ahead, axis, behind)
            by_offset[step] = from_ahead
    stacked = jnp.stack(by_offset)
    doubled = jnp.concatenate([stacked, stacked])
    return lax.dynamic_slice_in_dim(doubled, count - me, count, 0)


def ring_scatter(parts, axis):
    count = lax.axis_size(axis)
    me = lax.axis_index(axis)
    ahead = [(i, (i + 1) % count) for i in range(count)]
    behind = [(i, (i - 1) % count) for i in range(count)]
    far_behind = count // 2
    far_ahead = count - 1 - far_behind

    def block(offset):
        return lax.dynamic_index_in_dim(parts, (me + offset) % count, 0, keepdims=False).astype(jnp.float32)

    total = block(0)
    carry = None
    for step in range(far_behind):
        mine = block(far_behind - step)
        carry = mine if carry is None else carry + mine
        carry = lax.ppermute(carry.astype(jnp.bfloat16), axis, ahead).astype(jnp.float32)
    total = total + carry
    carry = None
    for step in range(far_ahead):
        mine = block(step - far_ahead)
        carry = mine if carry is None else carry + mine
        carry = lax.ppermute(carry.astype(jnp.bfloat16), axis, behind).astype(jnp.float32)
    return total + carry


def add_up(stack):
    total = stack[0].astype(jnp.float32)
    for index in range(1, stack.shape[0]):
        total = total + stack[index].astype(jnp.float32)
    return total


def gather_ch(local):
    chips = lax.axis_size("z")
    along_z = lax.all_to_all(jnp.broadcast_to(local[None], (chips,) + local.shape), "z", 0, 0, tiled=True)
    mine = lax.axis_index("core")
    other = swap_core(along_z)
    return jnp.stack([jnp.where(mine == 0, along_z, other), jnp.where(mine == 0, other, along_z)])


def scatter_ch(parts):
    mine = lax.axis_index("core")
    keep = jnp.where(mine == 0, parts[:, 0], parts[:, 1])
    send = jnp.where(mine == 0, parts[:, 1], parts[:, 0])
    on_chip = (keep.astype(jnp.float32) + swap_core(send).astype(jnp.float32)).astype(jnp.bfloat16)
    return add_up(lax.all_to_all(on_chip, "z", 0, 0, tiled=True))


def scatter_ch_offloaded(parts):
    mine = lax.axis_index("core")
    keep = jnp.where(mine == 0, parts[:, 0], parts[:, 1])
    send = jnp.where(mine == 0, parts[:, 1], parts[:, 0])
    on_chip = (keep.astype(jnp.float32) + swap_core(send).astype(jnp.float32)).astype(jnp.bfloat16)
    return lax.psum_scatter(on_chip, "z", scatter_dimension=0, tiled=True)[0].astype(jnp.float32)


def sum_rows(piece):
    bands = lax.axis_size("row")
    lanes = piece.shape[-1]
    packed = piece.astype(jnp.bfloat16).reshape(bands, -1, lanes)
    got = lax.all_to_all(packed, "row", 0, 0, tiled=True)
    reduced = add_up(got).astype(jnp.bfloat16)
    spread = jnp.broadcast_to(reduced[None], packed.shape)
    return lax.all_to_all(spread, "row", 0, 0, tiled=True).reshape(piece.shape)


def row_rims(local):
    padded = padded_2(local, (("row", 0),), 1)
    return jnp.pad(padded, ((0, 0), (1, 1), (0, 0)))


def group_view(local, group_width):
    return local.reshape(local.shape[0], local.shape[1], local.shape[2] // group_width, group_width)


def body(features, w_in, w_group, w_out, cotangent):
    row_count, col_count, local_ch = features.shape
    group_width = w_group.shape[2]
    local_mid = w_in.shape[1]
    pixel_count = row_count * col_count
    chips = lax.axis_size("z")
    cores = lax.axis_size("core")
    flat_local = features.reshape(pixel_count, local_ch)
    grad_flat = cotangent.reshape(pixel_count, local_ch)
    w_in_blocks = w_in.reshape(chips, cores, -1, local_mid)
    w_out_blocks = w_out.reshape(chips, cores, -1, local_ch)

    gathered = gather_ch(flat_local)
    pre_one = jnp.einsum("kzpc,zkcm->pm", gathered, w_in_blocks, preferred_element_type=jnp.float32)
    act_one = jax.nn.silu(pre_one).astype(jnp.bfloat16).reshape(row_count, col_count, local_mid)
    padded_one = group_view(row_rims(act_one), group_width)
    filters = w_group.reshape(3, 3, group_width, local_mid // group_width, group_width)
    pre_two = jnp.zeros((row_count, col_count, local_mid // group_width, group_width), jnp.float32)
    for row_tap in range(3):
        for col_tap in range(3):
            window = padded_one[row_tap : row_tap + row_count, col_tap : col_tap + col_count]
            pre_two = pre_two + jnp.einsum(
                "rcgi,igj->rcgj",
                window,
                filters[row_tap, col_tap],
                preferred_element_type=jnp.float32,
            )
    pre_two = pre_two.reshape(pixel_count, local_mid)
    act_two = jax.nn.silu(pre_two).astype(jnp.bfloat16)
    mid_full = gather_ch(act_two)
    branch = jnp.einsum("kzpm,zkmc->pc", mid_full, w_out_blocks, preferred_element_type=jnp.float32)
    block_out = (
        (flat_local.astype(jnp.float32) + branch)
        .astype(jnp.bfloat16)
        .reshape(row_count, col_count, local_ch)
    )
    two_parts = jnp.einsum(
        "pc,zkmc->zkpm", grad_flat, w_out_blocks, preferred_element_type=jnp.float32
    ).astype(jnp.bfloat16)
    d_two = scatter_ch_offloaded(two_parts)
    grad_two = (d_two * silu_slope(pre_two)).astype(jnp.bfloat16)
    padded_two = group_view(
        row_rims(grad_two.reshape(row_count, col_count, local_mid)), group_width
    )
    d_one = jnp.zeros((row_count, col_count, local_mid // group_width, group_width), jnp.float32)
    for row_tap in range(3):
        for col_tap in range(3):
            window = padded_two[
                2 - row_tap : 2 - row_tap + row_count, 2 - col_tap : 2 - col_tap + col_count
            ]
            d_one = d_one + jnp.einsum(
                "rcgj,igj->rcgi",
                window,
                filters[row_tap, col_tap],
                preferred_element_type=jnp.float32,
            )
    grad_one = (d_one.reshape(pixel_count, local_mid) * silu_slope(pre_one)).astype(jnp.bfloat16)
    grad_view = group_view(grad_two.reshape(row_count, col_count, local_mid), group_width)
    tap_rows = []
    for row_tap in range(3):
        tap_line = []
        for col_tap in range(3):
            window = padded_one[row_tap : row_tap + row_count, col_tap : col_tap + col_count]
            tap_line.append(
                jnp.einsum("rcgi,rcgj->igj", window, grad_view, preferred_element_type=jnp.float32)
            )
        tap_rows.append(jnp.stack(tap_line))
    group_grad = jnp.stack(tap_rows).reshape(3, 3, group_width, local_mid)
    in_grad = jnp.einsum("kzpc,pm->zkcm", gathered, grad_one, preferred_element_type=jnp.float32)
    out_grad = jnp.einsum("kzpm,pc->zkmc", mid_full, grad_flat, preferred_element_type=jnp.float32)
    one_parts = jnp.einsum(
        "pm,zkcm->zkpc", grad_one, w_in_blocks, preferred_element_type=jnp.float32
    ).astype(jnp.bfloat16)
    d_input = scatter_ch(one_parts)
    grad_input = (
        (grad_flat.astype(jnp.float32) + d_input)
        .astype(jnp.bfloat16)
        .reshape(row_count, col_count, local_ch)
    )
    outs = (
        sum_rows(in_grad),
        lax.psum(out_grad.astype(jnp.bfloat16), "row"),
        lax.psum(group_grad.astype(jnp.bfloat16), "row"),
    )
    return (
        block_out,
        grad_input,
        outs[0].reshape(-1, local_mid),
        outs[2],
        outs[1].reshape(-1, local_ch),
    )


def solution(mesh):
    rows, channels = mesh.devices.shape
    fine = Mesh(mesh.devices.reshape(rows, channels // 2, 2), ("row", "z", "core"))
    ch = ("z", "core")
    placed = (
        P("row", None, ch),
        P(None, ch),
        P(None, None, None, ch),
        P(None, ch),
        P("row", None, ch),
    )
    return jax.shard_map(
        body,
        mesh=fine,
        in_specs=placed,
        out_specs=(
            P("row", None, ch),
            P("row", None, ch),
            P(None, ch),
            P(None, None, None, ch),
            P(None, ch),
        ),
        check_vma=False,
    )
```

```python
import jax
import jax.numpy as jnp
from jax import lax
from jax.sharding import Mesh, PartitionSpec as P


def padded_2(cells, sides, width):
    for axis, dim in sides:
        count = lax.axis_size(axis)
        ends = count - 1
        head = lax.slice_in_dim(cells, 0, width, axis=dim)
        tail = lax.slice_in_dim(cells, cells.shape[dim] - width, cells.shape[dim], axis=dim)
        cells = jnp.concatenate(
            [
                lax.ppermute(tail, axis, [(i, (i + 1) % count) for i in range(ends)]),
                cells,
                lax.ppermute(head, axis, [((i + 1) % count, i) for i in range(ends)]),
            ],
            axis=dim,
        )
    return cells


def silu_slope(values):
    sigma = jax.nn.sigmoid(values)
    return sigma * (1.0 + values * (1.0 - sigma))


def swap_core(value):
    return lax.ppermute(value, "core", [(0, 1), (1, 0)])


def ring_gather(local, axis):
    count = lax.axis_size(axis)
    me = lax.axis_index(axis)
    ahead = [(i, (i + 1) % count) for i in range(count)]
    behind = [(i, (i - 1) % count) for i in range(count)]
    by_offset = [local] + [None] * (count - 1)
    from_behind = local
    from_ahead = local
    for step in range(1, count // 2 + 1):
        from_behind = lax.ppermute(from_behind, axis, ahead)
        by_offset[count - step] = from_behind
        if step < count - step:
            from_ahead = lax.ppermute(from_ahead, axis, behind)
            by_offset[step] = from_ahead
    stacked = jnp.stack(by_offset)
    doubled = jnp.concatenate([stacked, stacked])
    return lax.dynamic_slice_in_dim(doubled, count - me, count, 0)


def ring_scatter(parts, axis):
    count = lax.axis_size(axis)
    me = lax.axis_index(axis)
    ahead = [(i, (i + 1) % count) for i in range(count)]
    behind = [(i, (i - 1) % count) for i in range(count)]
    far_behind = count // 2
    far_ahead = count - 1 - far_behind

    def block(offset):
        return lax.dynamic_index_in_dim(parts, (me + offset) % count, 0, keepdims=False).astype(jnp.float32)

    total = block(0)
    carry = None
    for step in range(far_behind):
        mine = block(far_behind - step)
        carry = mine if carry is None else carry + mine
        carry = lax.ppermute(carry.astype(jnp.bfloat16), axis, ahead).astype(jnp.float32)
    total = total + carry
    carry = None
    for step in range(far_ahead):
        mine = block(step - far_ahead)
        carry = mine if carry is None else carry + mine
        carry = lax.ppermute(carry.astype(jnp.bfloat16), axis, behind).astype(jnp.float32)
    return total + carry


def add_up(stack):
    total = stack[0].astype(jnp.float32)
    for index in range(1, stack.shape[0]):
        total = total + stack[index].astype(jnp.float32)
    return total


def chip_sum(parts):
    mine = lax.axis_index("core")
    keep = jnp.where(mine == 0, parts[:, 0], parts[:, 1])
    send = jnp.where(mine == 0, parts[:, 1], parts[:, 0])
    return (keep.astype(jnp.float32) + swap_core(send).astype(jnp.float32)).astype(jnp.bfloat16)


def exchange_ch(local, parts):
    chips = lax.axis_size("z")
    spread = jnp.broadcast_to(local[None], (chips,) + local.shape)
    got = lax.all_to_all(jnp.stack([spread, chip_sum(parts)], axis=1), "z", 0, 0, tiled=True)
    along_z = got[:, 0]
    mine = lax.axis_index("core")
    other = swap_core(along_z)
    full = jnp.stack([jnp.where(mine == 0, along_z, other), jnp.where(mine == 0, other, along_z)])
    return full, add_up(got[:, 1])


def sum_rows(pieces):
    bands = lax.axis_size("row")
    lanes = pieces[0].shape[-1]
    flat = [piece.astype(jnp.bfloat16).reshape(-1, lanes) for piece in pieces]
    rows = sum(part.shape[0] for part in flat)
    unit = bands * 16
    padded_rows = (rows + unit - 1) // unit * unit
    flat.append(jnp.zeros((padded_rows - rows, lanes), jnp.bfloat16))
    packed = jnp.concatenate(flat).reshape(bands, padded_rows // bands, lanes)
    got = lax.all_to_all(packed, "row", 0, 0, tiled=True)
    reduced = add_up(got).astype(jnp.bfloat16)
    spread = jnp.broadcast_to(reduced[None], packed.shape)
    whole = lax.all_to_all(spread, "row", 0, 0, tiled=True).reshape(padded_rows, lanes)
    outs = []
    start = 0
    for piece in pieces:
        size = piece.size // lanes
        outs.append(whole[start : start + size].reshape(piece.shape))
        start += size
    return outs


def row_rims(local):
    padded = padded_2(local, (("row", 0),), 1)
    return jnp.pad(padded, ((0, 0), (1, 1), (0, 0)))


def group_view(local, group_width):
    return local.reshape(local.shape[0], local.shape[1], local.shape[2] // group_width, group_width)


def body(features, w_in, w_group, w_out, cotangent):
    row_count, col_count, local_ch = features.shape
    group_width = w_group.shape[2]
    local_mid = w_in.shape[1]
    pixel_count = row_count * col_count
    chips = lax.axis_size("z")
    cores = lax.axis_size("core")
    flat_local = features.reshape(pixel_count, local_ch)
    grad_flat = cotangent.reshape(pixel_count, local_ch)
    w_in_blocks = w_in.reshape(chips, cores, -1, local_mid)
    w_out_blocks = w_out.reshape(chips, cores, -1, local_ch)

    two_parts = jnp.einsum(
        "pc,zkmc->zkpm", grad_flat, w_out_blocks, preferred_element_type=jnp.float32
    ).astype(jnp.bfloat16)
    gathered, d_two = exchange_ch(flat_local, two_parts)
    pre_one = jnp.einsum("kzpc,zkcm->pm", gathered, w_in_blocks, preferred_element_type=jnp.float32)
    act_one = jax.nn.silu(pre_one).astype(jnp.bfloat16).reshape(row_count, col_count, local_mid)
    padded_one = group_view(row_rims(act_one), group_width)
    filters = w_group.reshape(3, 3, group_width, local_mid // group_width, group_width)
    pre_two = jnp.zeros((row_count, col_count, local_mid // group_width, group_width), jnp.float32)
    for row_tap in range(3):
        for col_tap in range(3):
            window = padded_one[row_tap : row_tap + row_count, col_tap : col_tap + col_count]
            pre_two = pre_two + jnp.einsum(
                "rcgi,igj->rcgj",
                window,
                filters[row_tap, col_tap],
                preferred_element_type=jnp.float32,
            )
    pre_two = pre_two.reshape(pixel_count, local_mid)
    act_two = jax.nn.silu(pre_two).astype(jnp.bfloat16)
    grad_two = (d_two * silu_slope(pre_two)).astype(jnp.bfloat16)
    padded_two = group_view(
        row_rims(grad_two.reshape(row_count, col_count, local_mid)), group_width
    )
    d_one = jnp.zeros((row_count, col_count, local_mid // group_width, group_width), jnp.float32)
    for row_tap in range(3):
        for col_tap in range(3):
            window = padded_two[
                2 - row_tap : 2 - row_tap + row_count, 2 - col_tap : 2 - col_tap + col_count
            ]
            d_one = d_one + jnp.einsum(
                "rcgj,igj->rcgi",
                window,
                filters[row_tap, col_tap],
                preferred_element_type=jnp.float32,
            )
    grad_one = (d_one.reshape(pixel_count, local_mid) * silu_slope(pre_one)).astype(jnp.bfloat16)
    grad_view = group_view(grad_two.reshape(row_count, col_count, local_mid), group_width)
    tap_rows = []
    for row_tap in range(3):
        tap_line = []
        for col_tap in range(3):
            window = padded_one[row_tap : row_tap + row_count, col_tap : col_tap + col_count]
            tap_line.append(
                jnp.einsum("rcgi,rcgj->igj", window, grad_view, preferred_element_type=jnp.float32)
            )
        tap_rows.append(jnp.stack(tap_line))
    group_grad = jnp.stack(tap_rows).reshape(3, 3, group_width, local_mid)
    one_parts = jnp.einsum(
        "pm,zkcm->zkpc", grad_one, w_in_blocks, preferred_element_type=jnp.float32
    ).astype(jnp.bfloat16)
    mid_full, d_input = exchange_ch(act_two, one_parts)
    branch = jnp.einsum("kzpm,zkmc->pc", mid_full, w_out_blocks, preferred_element_type=jnp.float32)
    block_out = (
        (flat_local.astype(jnp.float32) + branch)
        .astype(jnp.bfloat16)
        .reshape(row_count, col_count, local_ch)
    )
    in_grad = jnp.einsum("kzpc,pm->zkcm", gathered, grad_one, preferred_element_type=jnp.float32)
    out_grad = jnp.einsum("kzpm,pc->zkmc", mid_full, grad_flat, preferred_element_type=jnp.float32)
    grad_input = (
        (grad_flat.astype(jnp.float32) + d_input)
        .astype(jnp.bfloat16)
        .reshape(row_count, col_count, local_ch)
    )
    outs = sum_rows((in_grad, out_grad, group_grad))
    return (
        block_out,
        grad_input,
        outs[0].reshape(-1, local_mid),
        outs[2],
        outs[1].reshape(-1, local_ch),
    )


def solution(mesh):
    rows, channels = mesh.devices.shape
    fine = Mesh(mesh.devices.reshape(rows, channels // 2, 2), ("row", "z", "core"))
    ch = ("z", "core")
    placed = (
        P("row", None, ch),
        P(None, ch),
        P(None, None, None, ch),
        P(None, ch),
        P("row", None, ch),
    )
    return jax.shard_map(
        body,
        mesh=fine,
        in_specs=placed,
        out_specs=(
            P("row", None, ch),
            P("row", None, ch),
            P(None, ch),
            P(None, None, None, ch),
            P(None, ch),
        ),
        check_vma=False,
    )
```

```python
import jax
import jax.numpy as jnp
from jax import lax
from jax.sharding import Mesh, PartitionSpec as P


def padded_2(cells, sides, width):
    for axis, dim in sides:
        count = lax.axis_size(axis)
        ends = count - 1
        head = lax.slice_in_dim(cells, 0, width, axis=dim)
        tail = lax.slice_in_dim(cells, cells.shape[dim] - width, cells.shape[dim], axis=dim)
        cells = jnp.concatenate(
            [
                lax.ppermute(tail, axis, [(i, (i + 1) % count) for i in range(ends)]),
                cells,
                lax.ppermute(head, axis, [((i + 1) % count, i) for i in range(ends)]),
            ],
            axis=dim,
        )
    return cells


def silu_slope(values):
    sigma = jax.nn.sigmoid(values)
    return sigma * (1.0 + values * (1.0 - sigma))


def swap_core(value):
    return lax.ppermute(value, "core", [(0, 1), (1, 0)])


def add_up(stack):
    total = stack[0].astype(jnp.float32)
    for index in range(1, stack.shape[0]):
        total = total + stack[index].astype(jnp.float32)
    return total


def chip_sum(parts):
    mine = lax.axis_index("core")
    keep = jnp.where(mine == 0, parts[:, 0], parts[:, 1])
    send = jnp.where(mine == 0, parts[:, 1], parts[:, 0])
    return (keep.astype(jnp.float32) + swap_core(send).astype(jnp.float32)).astype(jnp.bfloat16)


def ring_exchange(local, parts, axis):
    count = lax.axis_size(axis)
    me = lax.axis_index(axis)
    ahead = [(i, (i + 1) % count) for i in range(count)]
    behind = [(i, (i - 1) % count) for i in range(count)]
    far_behind = count // 2
    far_ahead = count - 1 - far_behind

    def block(offset):
        return lax.dynamic_index_in_dim(parts, (me + offset) % count, 0, keepdims=False).astype(jnp.float32)

    by_offset = [local] + [None] * (count - 1)
    total = block(0)
    for hops, pairs, offset_of, block_of in (
        (far_behind, ahead, lambda s: count - s, lambda step: far_behind - step),
        (far_ahead, behind, lambda s: s, lambda step: step - far_ahead),
    ):
        chunk = local
        carry = None
        for step in range(hops):
            mine = block(block_of(step))
            carry = mine if carry is None else carry + mine
            got = lax.ppermute(jnp.stack([chunk, carry.astype(jnp.bfloat16)]), axis, pairs)
            chunk = got[0]
            carry = got[1].astype(jnp.float32)
            by_offset[offset_of(step + 1)] = chunk
        total = total + carry
    stacked = jnp.stack(by_offset)
    doubled = jnp.concatenate([stacked, stacked])
    return lax.dynamic_slice_in_dim(doubled, count - me, count, 0), total


def exchange_ch(local, parts):
    along_z, summed = ring_exchange(local, chip_sum(parts), "z")
    mine = lax.axis_index("core")
    other = swap_core(along_z)
    full = jnp.stack([jnp.where(mine == 0, along_z, other), jnp.where(mine == 0, other, along_z)])
    return full, summed


def sum_rows(pieces):
    bands = lax.axis_size("row")
    lanes = pieces[0].shape[-1]
    flat = [piece.astype(jnp.bfloat16).reshape(-1, lanes) for piece in pieces]
    rows = sum(part.shape[0] for part in flat)
    unit = bands * 16
    padded_rows = (rows + unit - 1) // unit * unit
    flat.append(jnp.zeros((padded_rows - rows, lanes), jnp.bfloat16))
    packed = jnp.concatenate(flat).reshape(bands, padded_rows // bands, lanes)
    got = lax.all_to_all(packed, "row", 0, 0, tiled=True)
    reduced = add_up(got).astype(jnp.bfloat16)
    spread = jnp.broadcast_to(reduced[None], packed.shape)
    whole = lax.all_to_all(spread, "row", 0, 0, tiled=True).reshape(padded_rows, lanes)
    outs = []
    start = 0
    for piece in pieces:
        size = piece.size // lanes
        outs.append(whole[start : start + size].reshape(piece.shape))
        start += size
    return outs


def row_rims(local):
    padded = padded_2(local, (("row", 0),), 1)
    return jnp.pad(padded, ((0, 0), (1, 1), (0, 0)))


def group_view(local, group_width):
    return local.reshape(local.shape[0], local.shape[1], local.shape[2] // group_width, group_width)


def body(features, w_in, w_group, w_out, cotangent):
    row_count, col_count, local_ch = features.shape
    group_width = w_group.shape[2]
    local_mid = w_in.shape[1]
    pixel_count = row_count * col_count
    chips = lax.axis_size("z")
    cores = lax.axis_size("core")
    flat_local = features.reshape(pixel_count, local_ch)
    grad_flat = cotangent.reshape(pixel_count, local_ch)
    w_in_blocks = w_in.reshape(chips, cores, -1, local_mid)
    w_out_blocks = w_out.reshape(chips, cores, -1, local_ch)

    two_parts = jnp.einsum(
        "pc,zkmc->zkpm", grad_flat, w_out_blocks, preferred_element_type=jnp.float32
    ).astype(jnp.bfloat16)
    gathered, d_two = exchange_ch(flat_local, two_parts)
    pre_one = jnp.einsum("kzpc,zkcm->pm", gathered, w_in_blocks, preferred_element_type=jnp.float32)
    act_one = jax.nn.silu(pre_one).astype(jnp.bfloat16).reshape(row_count, col_count, local_mid)
    padded_one = group_view(row_rims(act_one), group_width)
    filters = w_group.reshape(3, 3, group_width, local_mid // group_width, group_width)
    pre_two = jnp.zeros((row_count, col_count, local_mid // group_width, group_width), jnp.float32)
    for row_tap in range(3):
        for col_tap in range(3):
            window = padded_one[row_tap : row_tap + row_count, col_tap : col_tap + col_count]
            pre_two = pre_two + jnp.einsum(
                "rcgi,igj->rcgj",
                window,
                filters[row_tap, col_tap],
                preferred_element_type=jnp.float32,
            )
    pre_two = pre_two.reshape(pixel_count, local_mid)
    act_two = jax.nn.silu(pre_two).astype(jnp.bfloat16)
    grad_two = (d_two * silu_slope(pre_two)).astype(jnp.bfloat16)
    padded_two = group_view(
        row_rims(grad_two.reshape(row_count, col_count, local_mid)), group_width
    )
    d_one = jnp.zeros((row_count, col_count, local_mid // group_width, group_width), jnp.float32)
    for row_tap in range(3):
        for col_tap in range(3):
            window = padded_two[
                2 - row_tap : 2 - row_tap + row_count, 2 - col_tap : 2 - col_tap + col_count
            ]
            d_one = d_one + jnp.einsum(
                "rcgj,igj->rcgi",
                window,
                filters[row_tap, col_tap],
                preferred_element_type=jnp.float32,
            )
    grad_one = (d_one.reshape(pixel_count, local_mid) * silu_slope(pre_one)).astype(jnp.bfloat16)
    grad_view = group_view(grad_two.reshape(row_count, col_count, local_mid), group_width)
    tap_rows = []
    for row_tap in range(3):
        tap_line = []
        for col_tap in range(3):
            window = padded_one[row_tap : row_tap + row_count, col_tap : col_tap + col_count]
            tap_line.append(
                jnp.einsum("rcgi,rcgj->igj", window, grad_view, preferred_element_type=jnp.float32)
            )
        tap_rows.append(jnp.stack(tap_line))
    group_grad = jnp.stack(tap_rows).reshape(3, 3, group_width, local_mid)
    one_parts = jnp.einsum(
        "pm,zkcm->zkpc", grad_one, w_in_blocks, preferred_element_type=jnp.float32
    ).astype(jnp.bfloat16)
    mid_full, d_input = exchange_ch(act_two, one_parts)
    branch = jnp.einsum("kzpm,zkmc->pc", mid_full, w_out_blocks, preferred_element_type=jnp.float32)
    block_out = (
        (flat_local.astype(jnp.float32) + branch)
        .astype(jnp.bfloat16)
        .reshape(row_count, col_count, local_ch)
    )
    in_grad = jnp.einsum("kzpc,pm->zkcm", gathered, grad_one, preferred_element_type=jnp.float32)
    out_grad = jnp.einsum("kzpm,pc->zkmc", mid_full, grad_flat, preferred_element_type=jnp.float32)
    grad_input = (
        (grad_flat.astype(jnp.float32) + d_input)
        .astype(jnp.bfloat16)
        .reshape(row_count, col_count, local_ch)
    )
    outs = sum_rows((in_grad, out_grad, group_grad))
    return (
        block_out,
        grad_input,
        outs[0].reshape(-1, local_mid),
        outs[2],
        outs[1].reshape(-1, local_ch),
    )


def solution(mesh):
    rows, channels = mesh.devices.shape
    fine = Mesh(mesh.devices.reshape(rows, channels // 2, 2), ("row", "z", "core"))
    ch = ("z", "core")
    placed = (
        P("row", None, ch),
        P(None, ch),
        P(None, None, None, ch),
        P(None, ch),
        P("row", None, ch),
    )
    return jax.shard_map(
        body,
        mesh=fine,
        in_specs=placed,
        out_specs=(
            P("row", None, ch),
            P("row", None, ch),
            P(None, ch),
            P(None, None, None, ch),
            P(None, ch),
        ),
        check_vma=False,
    )
```

```python
import jax
import jax.numpy as jnp
from jax import lax
from jax.sharding import Mesh, PartitionSpec as P


def padded_2(cells, sides, width):
    for axis, dim in sides:
        count = lax.axis_size(axis)
        ends = count - 1
        head = lax.slice_in_dim(cells, 0, width, axis=dim)
        tail = lax.slice_in_dim(cells, cells.shape[dim] - width, cells.shape[dim], axis=dim)
        cells = jnp.concatenate(
            [
                lax.ppermute(tail, axis, [(i, (i + 1) % count) for i in range(ends)]),
                cells,
                lax.ppermute(head, axis, [((i + 1) % count, i) for i in range(ends)]),
            ],
            axis=dim,
        )
    return cells


def silu_slope(values):
    sigma = jax.nn.sigmoid(values)
    return sigma * (1.0 + values * (1.0 - sigma))


def swap_core(value):
    return lax.ppermute(value, "core", [(0, 1), (1, 0)])


def ring_scatter(parts, axis):
    count = lax.axis_size(axis)
    me = lax.axis_index(axis)
    ahead = [(i, (i + 1) % count) for i in range(count)]
    behind = [(i, (i - 1) % count) for i in range(count)]
    far_behind = count // 2
    far_ahead = count - 1 - far_behind

    def block(offset):
        return lax.dynamic_index_in_dim(parts, (me + offset) % count, 0, keepdims=False).astype(jnp.float32)

    total = block(0)
    carry = None
    for step in range(far_behind):
        mine = block(far_behind - step)
        carry = mine if carry is None else carry + mine
        carry = lax.ppermute(carry.astype(jnp.bfloat16), axis, ahead).astype(jnp.float32)
    total = total + carry
    carry = None
    for step in range(far_ahead):
        mine = block(step - far_ahead)
        carry = mine if carry is None else carry + mine
        carry = lax.ppermute(carry.astype(jnp.bfloat16), axis, behind).astype(jnp.float32)
    return total + carry


def add_up(stack):
    total = stack[0].astype(jnp.float32)
    for index in range(1, stack.shape[0]):
        total = total + stack[index].astype(jnp.float32)
    return total


def gather_ch(local):
    chips = lax.axis_size("z")
    along_z = lax.all_to_all(jnp.broadcast_to(local[None], (chips,) + local.shape), "z", 0, 0, tiled=True)
    mine = lax.axis_index("core")
    other = swap_core(along_z)
    return jnp.stack([jnp.where(mine == 0, along_z, other), jnp.where(mine == 0, other, along_z)])


def scatter_ch(parts):
    mine = lax.axis_index("core")
    keep = jnp.where(mine == 0, parts[:, 0], parts[:, 1])
    send = jnp.where(mine == 0, parts[:, 1], parts[:, 0])
    on_chip = (keep.astype(jnp.float32) + swap_core(send).astype(jnp.float32)).astype(jnp.bfloat16)
    return ring_scatter(on_chip, "z")


def sum_rows(pieces):
    bands = lax.axis_size("row")
    lanes = pieces[0].shape[-1]
    flat = [piece.astype(jnp.bfloat16).reshape(-1, lanes) for piece in pieces]
    rows = sum(part.shape[0] for part in flat)
    unit = bands * 16
    padded_rows = (rows + unit - 1) // unit * unit
    flat.append(jnp.zeros((padded_rows - rows, lanes), jnp.bfloat16))
    packed = jnp.concatenate(flat).reshape(bands, padded_rows // bands, lanes)
    got = lax.all_to_all(packed, "row", 0, 0, tiled=True)
    reduced = add_up(got).astype(jnp.bfloat16)
    spread = jnp.broadcast_to(reduced[None], packed.shape)
    whole = lax.all_to_all(spread, "row", 0, 0, tiled=True).reshape(padded_rows, lanes)
    outs = []
    start = 0
    for piece in pieces:
        size = piece.size // lanes
        outs.append(whole[start : start + size].reshape(piece.shape))
        start += size
    return outs


def row_rims(local):
    padded = padded_2(local, (("row", 0),), 1)
    return jnp.pad(padded, ((0, 0), (1, 1), (0, 0)))


def group_view(local, group_width):
    return local.reshape(local.shape[0], local.shape[1], local.shape[2] // group_width, group_width)


def body(features, w_in, w_group, w_out, cotangent):
    row_count, col_count, local_ch = features.shape
    group_width = w_group.shape[2]
    local_mid = w_in.shape[1]
    pixel_count = row_count * col_count
    chips = lax.axis_size("z")
    cores = lax.axis_size("core")
    flat_local = features.reshape(pixel_count, local_ch)
    grad_flat = cotangent.reshape(pixel_count, local_ch)
    w_in_blocks = w_in.reshape(chips, cores, -1, local_mid)
    w_out_blocks = w_out.reshape(chips, cores, -1, local_ch)

    gathered = gather_ch(flat_local)
    pre_one = jnp.einsum("kzpc,zkcm->pm", gathered, w_in_blocks, preferred_element_type=jnp.float32)
    act_one = jax.nn.silu(pre_one).astype(jnp.bfloat16).reshape(row_count, col_count, local_mid)
    padded_one = group_view(row_rims(act_one), group_width)
    filters = w_group.reshape(3, 3, group_width, local_mid // group_width, group_width)
    pre_two = jnp.zeros((row_count, col_count, local_mid // group_width, group_width), jnp.float32)
    for row_tap in range(3):
        for col_tap in range(3):
            window = padded_one[row_tap : row_tap + row_count, col_tap : col_tap + col_count]
            pre_two = pre_two + jnp.einsum(
                "rcgi,igj->rcgj",
                window,
                filters[row_tap, col_tap],
                preferred_element_type=jnp.float32,
            )
    pre_two = pre_two.reshape(pixel_count, local_mid)
    act_two = jax.nn.silu(pre_two).astype(jnp.bfloat16)
    mid_full = gather_ch(act_two)
    branch = jnp.einsum("kzpm,zkmc->pc", mid_full, w_out_blocks, preferred_element_type=jnp.float32)
    block_out = (
        (flat_local.astype(jnp.float32) + branch)
        .astype(jnp.bfloat16)
        .reshape(row_count, col_count, local_ch)
    )
    two_parts = jnp.einsum(
        "pc,zkmc->zkpm", grad_flat, w_out_blocks, preferred_element_type=jnp.float32
    ).astype(jnp.bfloat16)
    d_two = scatter_ch(two_parts)
    grad_two = (d_two * silu_slope(pre_two)).astype(jnp.bfloat16)
    padded_two = group_view(
        row_rims(grad_two.reshape(row_count, col_count, local_mid)), group_width
    )
    d_one = jnp.zeros((row_count, col_count, local_mid // group_width, group_width), jnp.float32)
    for row_tap in range(3):
        for col_tap in range(3):
            window = padded_two[
                2 - row_tap : 2 - row_tap + row_count, 2 - col_tap : 2 - col_tap + col_count
            ]
            d_one = d_one + jnp.einsum(
                "rcgj,igj->rcgi",
                window,
                filters[row_tap, col_tap],
                preferred_element_type=jnp.float32,
            )
    grad_one = (d_one.reshape(pixel_count, local_mid) * silu_slope(pre_one)).astype(jnp.bfloat16)
    grad_view = group_view(grad_two.reshape(row_count, col_count, local_mid), group_width)
    tap_rows = []
    for row_tap in range(3):
        tap_line = []
        for col_tap in range(3):
            window = padded_one[row_tap : row_tap + row_count, col_tap : col_tap + col_count]
            tap_line.append(
                jnp.einsum("rcgi,rcgj->igj", window, grad_view, preferred_element_type=jnp.float32)
            )
        tap_rows.append(jnp.stack(tap_line))
    group_grad = jnp.stack(tap_rows).reshape(3, 3, group_width, local_mid)
    in_grad = jnp.einsum("kzpc,pm->zkcm", gathered, grad_one, preferred_element_type=jnp.float32)
    out_grad = jnp.einsum("kzpm,pc->zkmc", mid_full, grad_flat, preferred_element_type=jnp.float32)
    one_parts = jnp.einsum(
        "pm,zkcm->zkpc", grad_one, w_in_blocks, preferred_element_type=jnp.float32
    ).astype(jnp.bfloat16)
    d_input = scatter_ch(one_parts)
    grad_input = (
        (grad_flat.astype(jnp.float32) + d_input)
        .astype(jnp.bfloat16)
        .reshape(row_count, col_count, local_ch)
    )
    outs = sum_rows((in_grad, out_grad, group_grad))
    return (
        block_out,
        grad_input,
        outs[0].reshape(-1, local_mid),
        outs[2],
        outs[1].reshape(-1, local_ch),
    )


def solution(mesh):
    rows, channels = mesh.devices.shape
    fine = Mesh(mesh.devices.reshape(rows, channels // 2, 2), ("row", "z", "core"))
    ch = ("z", "core")
    placed = (
        P("row", None, ch),
        P(None, ch),
        P(None, None, None, ch),
        P(None, ch),
        P("row", None, ch),
    )
    return jax.shard_map(
        body,
        mesh=fine,
        in_specs=placed,
        out_specs=(
            P("row", None, ch),
            P("row", None, ch),
            P(None, ch),
            P(None, None, None, ch),
            P(None, ch),
        ),
        check_vma=False,
    )
```

```python
import jax
import jax.numpy as jnp
from jax import lax
from jax.sharding import Mesh, PartitionSpec as P


def padded_2(cells, sides, width):
    for axis, dim in sides:
        count = lax.axis_size(axis)
        ends = count - 1
        head = lax.slice_in_dim(cells, 0, width, axis=dim)
        tail = lax.slice_in_dim(cells, cells.shape[dim] - width, cells.shape[dim], axis=dim)
        cells = jnp.concatenate(
            [
                lax.ppermute(tail, axis, [(i, (i + 1) % count) for i in range(ends)]),
                cells,
                lax.ppermute(head, axis, [((i + 1) % count, i) for i in range(ends)]),
            ],
            axis=dim,
        )
    return cells


def silu_slope(values):
    sigma = jax.nn.sigmoid(values)
    return sigma * (1.0 + values * (1.0 - sigma))


def swap_core(value):
    return lax.ppermute(value, "core", [(0, 1), (1, 0)])


def ring_scatter(parts, axis):
    count = lax.axis_size(axis)
    me = lax.axis_index(axis)
    ahead = [(i, (i + 1) % count) for i in range(count)]
    behind = [(i, (i - 1) % count) for i in range(count)]
    far_behind = count // 2
    far_ahead = count - 1 - far_behind

    def block(offset):
        return lax.dynamic_index_in_dim(parts, (me + offset) % count, 0, keepdims=False).astype(jnp.float32)

    total = block(0)
    carry = None
    for step in range(far_behind):
        mine = block(far_behind - step)
        carry = mine if carry is None else carry + mine
        carry = lax.ppermute(carry.astype(jnp.bfloat16), axis, ahead).astype(jnp.float32)
    total = total + carry
    carry = None
    for step in range(far_ahead):
        mine = block(step - far_ahead)
        carry = mine if carry is None else carry + mine
        carry = lax.ppermute(carry.astype(jnp.bfloat16), axis, behind).astype(jnp.float32)
    return total + carry


def add_up(stack):
    total = stack[0].astype(jnp.float32)
    for index in range(1, stack.shape[0]):
        total = total + stack[index].astype(jnp.float32)
    return total


def gather_ch(local):
    chips = lax.axis_size("z")
    along_z = lax.all_to_all(jnp.broadcast_to(local[None], (chips,) + local.shape), "z", 0, 0, tiled=True)
    mine = lax.axis_index("core")
    other = swap_core(along_z)
    return jnp.stack([jnp.where(mine == 0, along_z, other), jnp.where(mine == 0, other, along_z)])


def scatter_ch(parts):
    mine = lax.axis_index("core")
    keep = jnp.where(mine == 0, parts[:, 0], parts[:, 1])
    send = jnp.where(mine == 0, parts[:, 1], parts[:, 0])
    on_chip = (keep.astype(jnp.float32) + swap_core(send).astype(jnp.float32)).astype(jnp.bfloat16)
    return ring_scatter(on_chip, "z")


def sum_rows(pieces):
    bands = lax.axis_size("row")
    lanes = pieces[0].shape[-1]
    flat = [piece.astype(jnp.bfloat16).reshape(-1, lanes) for piece in pieces]
    rows = sum(part.shape[0] for part in flat)
    unit = bands * 16
    padded_rows = (rows + unit - 1) // unit * unit
    packed = jnp.zeros((padded_rows, lanes), jnp.bfloat16)
    start = 0
    for part in flat:
        packed = lax.dynamic_update_slice_in_dim(packed, part, start, 0)
        start += part.shape[0]
    packed = packed.reshape(bands, padded_rows // bands, lanes)
    got = lax.all_to_all(packed, "row", 0, 0, tiled=True)
    reduced = add_up(got).astype(jnp.bfloat16)
    spread = jnp.broadcast_to(reduced[None], packed.shape)
    whole = lax.all_to_all(spread, "row", 0, 0, tiled=True).reshape(padded_rows, lanes)
    outs = []
    start = 0
    for piece in pieces:
        size = piece.size // lanes
        outs.append(whole[start : start + size].reshape(piece.shape))
        start += size
    return outs


def row_rims(local):
    padded = padded_2(local, (("row", 0),), 1)
    return jnp.pad(padded, ((0, 0), (1, 1), (0, 0)))


def group_view(local, group_width):
    return local.reshape(local.shape[0], local.shape[1], local.shape[2] // group_width, group_width)


def body(features, w_in, w_group, w_out, cotangent):
    row_count, col_count, local_ch = features.shape
    group_width = w_group.shape[2]
    local_mid = w_in.shape[1]
    pixel_count = row_count * col_count
    chips = lax.axis_size("z")
    cores = lax.axis_size("core")
    flat_local = features.reshape(pixel_count, local_ch)
    grad_flat = cotangent.reshape(pixel_count, local_ch)
    w_in_blocks = w_in.reshape(chips, cores, -1, local_mid)
    w_out_blocks = w_out.reshape(chips, cores, -1, local_ch)

    gathered = gather_ch(flat_local)
    pre_one = jnp.einsum("kzpc,zkcm->pm", gathered, w_in_blocks, preferred_element_type=jnp.float32)
    act_one = jax.nn.silu(pre_one).astype(jnp.bfloat16).reshape(row_count, col_count, local_mid)
    padded_one = group_view(row_rims(act_one), group_width)
    filters = w_group.reshape(3, 3, group_width, local_mid // group_width, group_width)
    pre_two = jnp.zeros((row_count, col_count, local_mid // group_width, group_width), jnp.float32)
    for row_tap in range(3):
        for col_tap in range(3):
            window = padded_one[row_tap : row_tap + row_count, col_tap : col_tap + col_count]
            pre_two = pre_two + jnp.einsum(
                "rcgi,igj->rcgj",
                window,
                filters[row_tap, col_tap],
                preferred_element_type=jnp.float32,
            )
    pre_two = pre_two.reshape(pixel_count, local_mid)
    act_two = jax.nn.silu(pre_two).astype(jnp.bfloat16)
    mid_full = gather_ch(act_two)
    branch = jnp.einsum("kzpm,zkmc->pc", mid_full, w_out_blocks, preferred_element_type=jnp.float32)
    block_out = (
        (flat_local.astype(jnp.float32) + branch)
        .astype(jnp.bfloat16)
        .reshape(row_count, col_count, local_ch)
    )
    two_parts = jnp.einsum(
        "pc,zkmc->zkpm", grad_flat, w_out_blocks, preferred_element_type=jnp.float32
    ).astype(jnp.bfloat16)
    d_two = scatter_ch(two_parts)
    grad_two = (d_two * silu_slope(pre_two)).astype(jnp.bfloat16)
    padded_two = group_view(
        row_rims(grad_two.reshape(row_count, col_count, local_mid)), group_width
    )
    d_one = jnp.zeros((row_count, col_count, local_mid // group_width, group_width), jnp.float32)
    for row_tap in range(3):
        for col_tap in range(3):
            window = padded_two[
                2 - row_tap : 2 - row_tap + row_count, 2 - col_tap : 2 - col_tap + col_count
            ]
            d_one = d_one + jnp.einsum(
                "rcgj,igj->rcgi",
                window,
                filters[row_tap, col_tap],
                preferred_element_type=jnp.float32,
            )
    grad_one = (d_one.reshape(pixel_count, local_mid) * silu_slope(pre_one)).astype(jnp.bfloat16)
    grad_view = group_view(grad_two.reshape(row_count, col_count, local_mid), group_width)
    tap_rows = []
    for row_tap in range(3):
        tap_line = []
        for col_tap in range(3):
            window = padded_one[row_tap : row_tap + row_count, col_tap : col_tap + col_count]
            tap_line.append(
                jnp.einsum("rcgi,rcgj->igj", window, grad_view, preferred_element_type=jnp.float32)
            )
        tap_rows.append(jnp.stack(tap_line))
    group_grad = jnp.stack(tap_rows).reshape(3, 3, group_width, local_mid)
    in_grad = jnp.einsum("kzpc,pm->zkcm", gathered, grad_one, preferred_element_type=jnp.float32)
    out_grad = jnp.einsum("kzpm,pc->zkmc", mid_full, grad_flat, preferred_element_type=jnp.float32)
    one_parts = jnp.einsum(
        "pm,zkcm->zkpc", grad_one, w_in_blocks, preferred_element_type=jnp.float32
    ).astype(jnp.bfloat16)
    d_input = scatter_ch(one_parts)
    grad_input = (
        (grad_flat.astype(jnp.float32) + d_input)
        .astype(jnp.bfloat16)
        .reshape(row_count, col_count, local_ch)
    )
    outs = sum_rows((in_grad, out_grad, group_grad))
    return (
        block_out,
        grad_input,
        outs[0].reshape(-1, local_mid),
        outs[2],
        outs[1].reshape(-1, local_ch),
    )


def solution(mesh):
    rows, channels = mesh.devices.shape
    fine = Mesh(mesh.devices.reshape(rows, channels // 2, 2), ("row", "z", "core"))
    ch = ("z", "core")
    placed = (
        P("row", None, ch),
        P(None, ch),
        P(None, None, None, ch),
        P(None, ch),
        P("row", None, ch),
    )
    return jax.shard_map(
        body,
        mesh=fine,
        in_specs=placed,
        out_specs=(
            P("row", None, ch),
            P("row", None, ch),
            P(None, ch),
            P(None, None, None, ch),
            P(None, ch),
        ),
        check_vma=False,
    )
```

```python
import jax
import jax.numpy as jnp
from jax import lax
from jax.sharding import Mesh, PartitionSpec as P


def padded_2(cells, sides, width):
    for axis, dim in sides:
        count = lax.axis_size(axis)
        ends = count - 1
        head = lax.slice_in_dim(cells, 0, width, axis=dim)
        tail = lax.slice_in_dim(cells, cells.shape[dim] - width, cells.shape[dim], axis=dim)
        cells = jnp.concatenate(
            [
                lax.ppermute(tail, axis, [(i, (i + 1) % count) for i in range(ends)]),
                cells,
                lax.ppermute(head, axis, [((i + 1) % count, i) for i in range(ends)]),
            ],
            axis=dim,
        )
    return cells


def silu_slope(values):
    sigma = jax.nn.sigmoid(values)
    return sigma * (1.0 + values * (1.0 - sigma))


def swap_core(value):
    return lax.ppermute(value, "core", [(0, 1), (1, 0)])


def ring_scatter(parts, axis):
    count = lax.axis_size(axis)
    me = lax.axis_index(axis)
    ahead = [(i, (i + 1) % count) for i in range(count)]
    behind = [(i, (i - 1) % count) for i in range(count)]
    far_behind = count // 2
    far_ahead = count - 1 - far_behind

    def block(offset):
        return lax.dynamic_index_in_dim(parts, (me + offset) % count, 0, keepdims=False).astype(jnp.float32)

    total = block(0)
    carry = None
    for step in range(far_behind):
        mine = block(far_behind - step)
        carry = mine if carry is None else carry + mine
        carry = lax.ppermute(carry.astype(jnp.bfloat16), axis, ahead).astype(jnp.float32)
    total = total + carry
    carry = None
    for step in range(far_ahead):
        mine = block(step - far_ahead)
        carry = mine if carry is None else carry + mine
        carry = lax.ppermute(carry.astype(jnp.bfloat16), axis, behind).astype(jnp.float32)
    return total + carry


def add_up(stack):
    total = stack[0].astype(jnp.float32)
    for index in range(1, stack.shape[0]):
        total = total + stack[index].astype(jnp.float32)
    return total


def gather_ch(local):
    chips = lax.axis_size("z")
    along_z = lax.all_to_all(jnp.broadcast_to(local[None], (chips,) + local.shape), "z", 0, 0, tiled=True)
    mine = lax.axis_index("core")
    other = swap_core(along_z)
    return jnp.stack([jnp.where(mine == 0, along_z, other), jnp.where(mine == 0, other, along_z)])


def scatter_ch(parts, by_ring):
    mine = lax.axis_index("core")
    keep = jnp.where(mine == 0, parts[:, 0], parts[:, 1])
    send = jnp.where(mine == 0, parts[:, 1], parts[:, 0])
    on_chip = (keep.astype(jnp.float32) + swap_core(send).astype(jnp.float32)).astype(jnp.bfloat16)
    if by_ring:
        return ring_scatter(on_chip, "z")
    return add_up(lax.all_to_all(on_chip, "z", 0, 0, tiled=True))


def sum_rows(pieces):
    bands = lax.axis_size("row")
    lanes = pieces[0].shape[-1]
    flat = [piece.astype(jnp.bfloat16).reshape(-1, lanes) for piece in pieces]
    rows = sum(part.shape[0] for part in flat)
    unit = bands * 16
    padded_rows = (rows + unit - 1) // unit * unit
    packed = jnp.zeros((padded_rows, lanes), jnp.bfloat16)
    start = 0
    for part in flat:
        packed = lax.dynamic_update_slice_in_dim(packed, part, start, 0)
        start += part.shape[0]
    packed = packed.reshape(bands, padded_rows // bands, lanes)
    got = lax.all_to_all(packed, "row", 0, 0, tiled=True)
    reduced = add_up(got).astype(jnp.bfloat16)
    spread = jnp.broadcast_to(reduced[None], packed.shape)
    whole = lax.all_to_all(spread, "row", 0, 0, tiled=True).reshape(padded_rows, lanes)
    outs = []
    start = 0
    for piece in pieces:
        size = piece.size // lanes
        outs.append(whole[start : start + size].reshape(piece.shape))
        start += size
    return outs


def row_rims(local):
    padded = padded_2(local, (("row", 0),), 1)
    return jnp.pad(padded, ((0, 0), (1, 1), (0, 0)))


def group_view(local, group_width):
    return local.reshape(local.shape[0], local.shape[1], local.shape[2] // group_width, group_width)


def body(features, w_in, w_group, w_out, cotangent):
    row_count, col_count, local_ch = features.shape
    group_width = w_group.shape[2]
    local_mid = w_in.shape[1]
    pixel_count = row_count * col_count
    chips = lax.axis_size("z")
    cores = lax.axis_size("core")
    flat_local = features.reshape(pixel_count, local_ch)
    grad_flat = cotangent.reshape(pixel_count, local_ch)
    w_in_blocks = w_in.reshape(chips, cores, -1, local_mid)
    w_out_blocks = w_out.reshape(chips, cores, -1, local_ch)

    gathered = gather_ch(flat_local)
    pre_one = jnp.einsum("kzpc,zkcm->pm", gathered, w_in_blocks, preferred_element_type=jnp.float32)
    act_one = jax.nn.silu(pre_one).astype(jnp.bfloat16).reshape(row_count, col_count, local_mid)
    padded_one = group_view(row_rims(act_one), group_width)
    filters = w_group.reshape(3, 3, group_width, local_mid // group_width, group_width)
    pre_two = jnp.zeros((row_count, col_count, local_mid // group_width, group_width), jnp.float32)
    for row_tap in range(3):
        for col_tap in range(3):
            window = padded_one[row_tap : row_tap + row_count, col_tap : col_tap + col_count]
            pre_two = pre_two + jnp.einsum(
                "rcgi,igj->rcgj",
                window,
                filters[row_tap, col_tap],
                preferred_element_type=jnp.float32,
            )
    pre_two = pre_two.reshape(pixel_count, local_mid)
    act_two = jax.nn.silu(pre_two).astype(jnp.bfloat16)
    mid_full = gather_ch(act_two)
    branch = jnp.einsum("kzpm,zkmc->pc", mid_full, w_out_blocks, preferred_element_type=jnp.float32)
    block_out = (
        (flat_local.astype(jnp.float32) + branch)
        .astype(jnp.bfloat16)
        .reshape(row_count, col_count, local_ch)
    )
    two_parts = jnp.einsum(
        "pc,zkmc->zkpm", grad_flat, w_out_blocks, preferred_element_type=jnp.float32
    ).astype(jnp.bfloat16)
    d_two = scatter_ch(two_parts, False)
    grad_two = (d_two * silu_slope(pre_two)).astype(jnp.bfloat16)
    padded_two = group_view(
        row_rims(grad_two.reshape(row_count, col_count, local_mid)), group_width
    )
    d_one = jnp.zeros((row_count, col_count, local_mid // group_width, group_width), jnp.float32)
    for row_tap in range(3):
        for col_tap in range(3):
            window = padded_two[
                2 - row_tap : 2 - row_tap + row_count, 2 - col_tap : 2 - col_tap + col_count
            ]
            d_one = d_one + jnp.einsum(
                "rcgj,igj->rcgi",
                window,
                filters[row_tap, col_tap],
                preferred_element_type=jnp.float32,
            )
    grad_one = (d_one.reshape(pixel_count, local_mid) * silu_slope(pre_one)).astype(jnp.bfloat16)
    grad_view = group_view(grad_two.reshape(row_count, col_count, local_mid), group_width)
    tap_rows = []
    for row_tap in range(3):
        tap_line = []
        for col_tap in range(3):
            window = padded_one[row_tap : row_tap + row_count, col_tap : col_tap + col_count]
            tap_line.append(
                jnp.einsum("rcgi,rcgj->igj", window, grad_view, preferred_element_type=jnp.float32)
            )
        tap_rows.append(jnp.stack(tap_line))
    group_grad = jnp.stack(tap_rows).reshape(3, 3, group_width, local_mid)
    in_grad = jnp.einsum("kzpc,pm->zkcm", gathered, grad_one, preferred_element_type=jnp.float32)
    out_grad = jnp.einsum("kzpm,pc->zkmc", mid_full, grad_flat, preferred_element_type=jnp.float32)
    one_parts = jnp.einsum(
        "pm,zkcm->zkpc", grad_one, w_in_blocks, preferred_element_type=jnp.float32
    ).astype(jnp.bfloat16)
    d_input = scatter_ch(one_parts, True)
    grad_input = (
        (grad_flat.astype(jnp.float32) + d_input)
        .astype(jnp.bfloat16)
        .reshape(row_count, col_count, local_ch)
    )
    outs = sum_rows((in_grad, out_grad, group_grad))
    return (
        block_out,
        grad_input,
        outs[0].reshape(-1, local_mid),
        outs[2],
        outs[1].reshape(-1, local_ch),
    )


def solution(mesh):
    rows, channels = mesh.devices.shape
    fine = Mesh(mesh.devices.reshape(rows, channels // 2, 2), ("row", "z", "core"))
    ch = ("z", "core")
    placed = (
        P("row", None, ch),
        P(None, ch),
        P(None, None, None, ch),
        P(None, ch),
        P("row", None, ch),
    )
    return jax.shard_map(
        body,
        mesh=fine,
        in_specs=placed,
        out_specs=(
            P("row", None, ch),
            P("row", None, ch),
            P(None, ch),
            P(None, None, None, ch),
            P(None, ch),
        ),
        check_vma=False,
    )
```

```python
import jax
import jax.numpy as jnp
from jax import lax
from jax.sharding import Mesh, PartitionSpec as P


def padded_2(cells, sides, width):
    for axis, dim in sides:
        count = lax.axis_size(axis)
        ends = count - 1
        head = lax.slice_in_dim(cells, 0, width, axis=dim)
        tail = lax.slice_in_dim(cells, cells.shape[dim] - width, cells.shape[dim], axis=dim)
        cells = jnp.concatenate(
            [
                lax.ppermute(tail, axis, [(i, (i + 1) % count) for i in range(ends)]),
                cells,
                lax.ppermute(head, axis, [((i + 1) % count, i) for i in range(ends)]),
            ],
            axis=dim,
        )
    return cells


def silu_slope(values):
    sigma = jax.nn.sigmoid(values)
    return sigma * (1.0 + values * (1.0 - sigma))


def swap_core(value):
    return lax.ppermute(value, "core", [(0, 1), (1, 0)])


def ring_scatter(parts, axis, tied, tie_step):
    count = lax.axis_size(axis)
    me = lax.axis_index(axis)
    ahead = [(i, (i + 1) % count) for i in range(count)]
    behind = [(i, (i - 1) % count) for i in range(count)]
    far_behind = count // 2
    far_ahead = count - 1 - far_behind

    def block(offset):
        return lax.dynamic_index_in_dim(parts, (me + offset) % count, 0, keepdims=False).astype(jnp.float32)

    def hop(carry, mine, pairs):
        carry = mine if carry is None else carry + mine
        return lax.ppermute(carry.astype(jnp.bfloat16), axis, pairs).astype(jnp.float32)

    forward = None
    backward = None
    for step in range(max(far_behind, far_ahead)):
        if step < far_behind:
            forward = hop(forward, block(far_behind - step), ahead)
        if step < far_ahead:
            backward = hop(backward, block(step - far_ahead), behind)
        if step == tie_step:
            tied, forward, backward = lax.optimization_barrier((tied, forward, backward))
    return block(0) + forward + backward, tied


def add_up(stack):
    total = stack[0].astype(jnp.float32)
    for index in range(1, stack.shape[0]):
        total = total + stack[index].astype(jnp.float32)
    return total


def gather_ch(local):
    chips = lax.axis_size("z")
    along_z = lax.all_to_all(jnp.broadcast_to(local[None], (chips,) + local.shape), "z", 0, 0, tiled=True)
    mine = lax.axis_index("core")
    other = swap_core(along_z)
    return jnp.stack([jnp.where(mine == 0, along_z, other), jnp.where(mine == 0, other, along_z)])


def chip_sum(parts):
    mine = lax.axis_index("core")
    keep = jnp.where(mine == 0, parts[:, 0], parts[:, 1])
    send = jnp.where(mine == 0, parts[:, 1], parts[:, 0])
    return (keep.astype(jnp.float32) + swap_core(send).astype(jnp.float32)).astype(jnp.bfloat16)


def scatter_ch(parts):
    mine = lax.axis_index("core")
    keep = jnp.where(mine == 0, parts[:, 0], parts[:, 1])
    send = jnp.where(mine == 0, parts[:, 1], parts[:, 0])
    on_chip = (keep.astype(jnp.float32) + swap_core(send).astype(jnp.float32)).astype(jnp.bfloat16)
    return add_up(lax.all_to_all(on_chip, "z", 0, 0, tiled=True))


def sum_rows(pieces):
    bands = lax.axis_size("row")
    lanes = pieces[0].shape[-1]
    flat = [piece.astype(jnp.bfloat16).reshape(-1, lanes) for piece in pieces]
    rows = sum(part.shape[0] for part in flat)
    unit = bands * 16
    padded_rows = (rows + unit - 1) // unit * unit
    packed = jnp.zeros((padded_rows, lanes), jnp.bfloat16)
    start = 0
    for part in flat:
        packed = lax.dynamic_update_slice_in_dim(packed, part, start, 0)
        start += part.shape[0]
    packed = packed.reshape(bands, padded_rows // bands, lanes)
    got = lax.all_to_all(packed, "row", 0, 0, tiled=True)
    reduced = add_up(got).astype(jnp.bfloat16)
    spread = jnp.broadcast_to(reduced[None], packed.shape)
    whole = lax.all_to_all(spread, "row", 0, 0, tiled=True).reshape(padded_rows, lanes)
    outs = []
    start = 0
    for piece in pieces:
        size = piece.size // lanes
        outs.append(whole[start : start + size].reshape(piece.shape))
        start += size
    return outs


def row_rims(local):
    padded = padded_2(local, (("row", 0),), 1)
    return jnp.pad(padded, ((0, 0), (1, 1), (0, 0)))


def group_view(local, group_width):
    return local.reshape(local.shape[0], local.shape[1], local.shape[2] // group_width, group_width)


def body(features, w_in, w_group, w_out, cotangent):
    row_count, col_count, local_ch = features.shape
    group_width = w_group.shape[2]
    local_mid = w_in.shape[1]
    pixel_count = row_count * col_count
    chips = lax.axis_size("z")
    cores = lax.axis_size("core")
    flat_local = features.reshape(pixel_count, local_ch)
    grad_flat = cotangent.reshape(pixel_count, local_ch)
    w_in_blocks = w_in.reshape(chips, cores, -1, local_mid)
    w_out_blocks = w_out.reshape(chips, cores, -1, local_ch)

    gathered = gather_ch(flat_local)
    pre_one = jnp.einsum("kzpc,zkcm->pm", gathered, w_in_blocks, preferred_element_type=jnp.float32)
    act_one = jax.nn.silu(pre_one).astype(jnp.bfloat16).reshape(row_count, col_count, local_mid)
    padded_one = group_view(row_rims(act_one), group_width)
    filters = w_group.reshape(3, 3, group_width, local_mid // group_width, group_width)
    pre_two = jnp.zeros((row_count, col_count, local_mid // group_width, group_width), jnp.float32)
    for row_tap in range(3):
        for col_tap in range(3):
            window = padded_one[row_tap : row_tap + row_count, col_tap : col_tap + col_count]
            pre_two = pre_two + jnp.einsum(
                "rcgi,igj->rcgj",
                window,
                filters[row_tap, col_tap],
                preferred_element_type=jnp.float32,
            )
    pre_two = pre_two.reshape(pixel_count, local_mid)
    act_two = jax.nn.silu(pre_two).astype(jnp.bfloat16)
    mid_full = gather_ch(act_two)
    branch = jnp.einsum("kzpm,zkmc->pc", mid_full, w_out_blocks, preferred_element_type=jnp.float32)
    block_out = (
        (flat_local.astype(jnp.float32) + branch)
        .astype(jnp.bfloat16)
        .reshape(row_count, col_count, local_ch)
    )
    two_parts = jnp.einsum(
        "pc,zkmc->zkpm", grad_flat, w_out_blocks, preferred_element_type=jnp.float32
    ).astype(jnp.bfloat16)
    d_two = scatter_ch(two_parts)
    grad_two = (d_two * silu_slope(pre_two)).astype(jnp.bfloat16)
    padded_two = group_view(
        row_rims(grad_two.reshape(row_count, col_count, local_mid)), group_width
    )
    d_one = jnp.zeros((row_count, col_count, local_mid // group_width, group_width), jnp.float32)
    for row_tap in range(3):
        for col_tap in range(3):
            window = padded_two[
                2 - row_tap : 2 - row_tap + row_count, 2 - col_tap : 2 - col_tap + col_count
            ]
            d_one = d_one + jnp.einsum(
                "rcgj,igj->rcgi",
                window,
                filters[row_tap, col_tap],
                preferred_element_type=jnp.float32,
            )
    grad_one = (d_one.reshape(pixel_count, local_mid) * silu_slope(pre_one)).astype(jnp.bfloat16)
    grad_view = group_view(grad_two.reshape(row_count, col_count, local_mid), group_width)
    tap_rows = []
    for row_tap in range(3):
        tap_line = []
        for col_tap in range(3):
            window = padded_one[row_tap : row_tap + row_count, col_tap : col_tap + col_count]
            tap_line.append(
                jnp.einsum("rcgi,rcgj->igj", window, grad_view, preferred_element_type=jnp.float32)
            )
        tap_rows.append(jnp.stack(tap_line))
    group_grad = jnp.stack(tap_rows).reshape(3, 3, group_width, local_mid)
    in_grad = jnp.einsum("kzpc,pm->zkcm", gathered, grad_one, preferred_element_type=jnp.float32)
    one_parts = jnp.einsum(
        "pm,zkcm->zkpc", grad_one, w_in_blocks, preferred_element_type=jnp.float32
    ).astype(jnp.bfloat16)
    d_input, mid_full = ring_scatter(chip_sum(one_parts), "z", mid_full, 3)
    out_grad = jnp.einsum("kzpm,pc->zkmc", mid_full, grad_flat, preferred_element_type=jnp.float32)
    grad_input = (
        (grad_flat.astype(jnp.float32) + d_input)
        .astype(jnp.bfloat16)
        .reshape(row_count, col_count, local_ch)
    )
    outs = sum_rows((in_grad, out_grad, group_grad))
    return (
        block_out,
        grad_input,
        outs[0].reshape(-1, local_mid),
        outs[2],
        outs[1].reshape(-1, local_ch),
    )


def solution(mesh):
    rows, channels = mesh.devices.shape
    fine = Mesh(mesh.devices.reshape(rows, channels // 2, 2), ("row", "z", "core"))
    ch = ("z", "core")
    placed = (
        P("row", None, ch),
        P(None, ch),
        P(None, None, None, ch),
        P(None, ch),
        P("row", None, ch),
    )
    return jax.shard_map(
        body,
        mesh=fine,
        in_specs=placed,
        out_specs=(
            P("row", None, ch),
            P("row", None, ch),
            P(None, ch),
            P(None, None, None, ch),
            P(None, ch),
        ),
        check_vma=False,
    )
```

```python
import jax
import jax.numpy as jnp
from jax import lax
from jax.sharding import Mesh, PartitionSpec as P


def padded_2(cells, sides, width):
    for axis, dim in sides:
        count = lax.axis_size(axis)
        ends = count - 1
        head = lax.slice_in_dim(cells, 0, width, axis=dim)
        tail = lax.slice_in_dim(cells, cells.shape[dim] - width, cells.shape[dim], axis=dim)
        cells = jnp.concatenate(
            [
                lax.ppermute(tail, axis, [(i, (i + 1) % count) for i in range(ends)]),
                cells,
                lax.ppermute(head, axis, [((i + 1) % count, i) for i in range(ends)]),
            ],
            axis=dim,
        )
    return cells


def silu_slope(values):
    sigma = jax.nn.sigmoid(values)
    return sigma * (1.0 + values * (1.0 - sigma))


def swap_core(value):
    return lax.ppermute(value, "core", [(0, 1), (1, 0)])


def ring_scatter(parts, axis):
    count = lax.axis_size(axis)
    me = lax.axis_index(axis)
    ahead = [(i, (i + 1) % count) for i in range(count)]
    behind = [(i, (i - 1) % count) for i in range(count)]
    far_behind = count // 2
    far_ahead = count - 1 - far_behind

    def block(offset):
        return lax.dynamic_index_in_dim(parts, (me + offset) % count, 0, keepdims=False).astype(jnp.float32)

    total = block(0)
    carry = None
    for step in range(far_behind):
        mine = block(far_behind - step)
        carry = mine if carry is None else carry + mine
        carry = lax.ppermute(carry.astype(jnp.bfloat16), axis, ahead).astype(jnp.float32)
    total = total + carry
    carry = None
    for step in range(far_ahead):
        mine = block(step - far_ahead)
        carry = mine if carry is None else carry + mine
        carry = lax.ppermute(carry.astype(jnp.bfloat16), axis, behind).astype(jnp.float32)
    return total + carry


def add_up(stack):
    total = stack[0].astype(jnp.float32)
    for index in range(1, stack.shape[0]):
        total = total + stack[index].astype(jnp.float32)
    return total


def gather_ch(local):
    chips = lax.axis_size("z")
    along_z = lax.all_to_all(jnp.broadcast_to(local[None], (chips,) + local.shape), "z", 0, 0, tiled=True)
    mine = lax.axis_index("core")
    other = swap_core(along_z)
    return jnp.stack([jnp.where(mine == 0, along_z, other), jnp.where(mine == 0, other, along_z)])


def scatter_ch(parts, by_ring):
    mine = lax.axis_index("core")
    keep = jnp.where(mine == 0, parts[:, 0], parts[:, 1])
    send = jnp.where(mine == 0, parts[:, 1], parts[:, 0])
    on_chip = (keep.astype(jnp.float32) + swap_core(send).astype(jnp.float32)).astype(jnp.bfloat16)
    if by_ring:
        return ring_scatter(on_chip, "z")
    return add_up(lax.all_to_all(on_chip, "z", 0, 0, tiled=True))


def sum_rows(pieces):
    bands = lax.axis_size("row")
    lanes = pieces[0].shape[-1]
    flat = [piece.astype(jnp.bfloat16).reshape(-1, lanes) for piece in pieces]
    rows = sum(part.shape[0] for part in flat)
    unit = bands * 16
    padded_rows = (rows + unit - 1) // unit * unit
    packed = jnp.zeros((padded_rows, lanes), jnp.bfloat16)
    start = 0
    for part in flat:
        packed = lax.dynamic_update_slice_in_dim(packed, part, start, 0)
        start += part.shape[0]
    packed = packed.reshape(bands, padded_rows // bands, lanes)
    got = lax.all_to_all(packed, "row", 0, 0, tiled=True)
    reduced = add_up(got).astype(jnp.bfloat16)
    whole = lax.all_gather(reduced, "row", axis=0, tiled=False).reshape(padded_rows, lanes)
    outs = []
    start = 0
    for piece in pieces:
        size = piece.size // lanes
        outs.append(whole[start : start + size].reshape(piece.shape))
        start += size
    return outs


def row_rims(local):
    padded = padded_2(local, (("row", 0),), 1)
    return jnp.pad(padded, ((0, 0), (1, 1), (0, 0)))


def group_view(local, group_width):
    return local.reshape(local.shape[0], local.shape[1], local.shape[2] // group_width, group_width)


def body(features, w_in, w_group, w_out, cotangent):
    row_count, col_count, local_ch = features.shape
    group_width = w_group.shape[2]
    local_mid = w_in.shape[1]
    pixel_count = row_count * col_count
    chips = lax.axis_size("z")
    cores = lax.axis_size("core")
    flat_local = features.reshape(pixel_count, local_ch)
    grad_flat = cotangent.reshape(pixel_count, local_ch)
    w_in_blocks = w_in.reshape(chips, cores, -1, local_mid)
    w_out_blocks = w_out.reshape(chips, cores, -1, local_ch)

    gathered = gather_ch(flat_local)
    pre_one = jnp.einsum("kzpc,zkcm->pm", gathered, w_in_blocks, preferred_element_type=jnp.float32)
    act_one = jax.nn.silu(pre_one).astype(jnp.bfloat16).reshape(row_count, col_count, local_mid)
    padded_one = group_view(row_rims(act_one), group_width)
    filters = w_group.reshape(3, 3, group_width, local_mid // group_width, group_width)
    pre_two = jnp.zeros((row_count, col_count, local_mid // group_width, group_width), jnp.float32)
    for row_tap in range(3):
        for col_tap in range(3):
            window = padded_one[row_tap : row_tap + row_count, col_tap : col_tap + col_count]
            pre_two = pre_two + jnp.einsum(
                "rcgi,igj->rcgj",
                window,
                filters[row_tap, col_tap],
                preferred_element_type=jnp.float32,
            )
    pre_two = pre_two.reshape(pixel_count, local_mid)
    act_two = jax.nn.silu(pre_two).astype(jnp.bfloat16)
    mid_full = gather_ch(act_two)
    branch = jnp.einsum("kzpm,zkmc->pc", mid_full, w_out_blocks, preferred_element_type=jnp.float32)
    block_out = (
        (flat_local.astype(jnp.float32) + branch)
        .astype(jnp.bfloat16)
        .reshape(row_count, col_count, local_ch)
    )
    two_parts = jnp.einsum(
        "pc,zkmc->zkpm", grad_flat, w_out_blocks, preferred_element_type=jnp.float32
    ).astype(jnp.bfloat16)
    d_two = scatter_ch(two_parts, False)
    grad_two = (d_two * silu_slope(pre_two)).astype(jnp.bfloat16)
    padded_two = group_view(
        row_rims(grad_two.reshape(row_count, col_count, local_mid)), group_width
    )
    d_one = jnp.zeros((row_count, col_count, local_mid // group_width, group_width), jnp.float32)
    for row_tap in range(3):
        for col_tap in range(3):
            window = padded_two[
                2 - row_tap : 2 - row_tap + row_count, 2 - col_tap : 2 - col_tap + col_count
            ]
            d_one = d_one + jnp.einsum(
                "rcgj,igj->rcgi",
                window,
                filters[row_tap, col_tap],
                preferred_element_type=jnp.float32,
            )
    grad_one = (d_one.reshape(pixel_count, local_mid) * silu_slope(pre_one)).astype(jnp.bfloat16)
    grad_view = group_view(grad_two.reshape(row_count, col_count, local_mid), group_width)
    tap_rows = []
    for row_tap in range(3):
        tap_line = []
        for col_tap in range(3):
            window = padded_one[row_tap : row_tap + row_count, col_tap : col_tap + col_count]
            tap_line.append(
                jnp.einsum("rcgi,rcgj->igj", window, grad_view, preferred_element_type=jnp.float32)
            )
        tap_rows.append(jnp.stack(tap_line))
    group_grad = jnp.stack(tap_rows).reshape(3, 3, group_width, local_mid)
    in_grad = jnp.einsum("kzpc,pm->zkcm", gathered, grad_one, preferred_element_type=jnp.float32)
    out_grad = jnp.einsum("kzpm,pc->zkmc", mid_full, grad_flat, preferred_element_type=jnp.float32)
    one_parts = jnp.einsum(
        "pm,zkcm->zkpc", grad_one, w_in_blocks, preferred_element_type=jnp.float32
    ).astype(jnp.bfloat16)
    d_input = scatter_ch(one_parts, True)
    grad_input = (
        (grad_flat.astype(jnp.float32) + d_input)
        .astype(jnp.bfloat16)
        .reshape(row_count, col_count, local_ch)
    )
    outs = sum_rows((in_grad, out_grad, group_grad))
    return (
        block_out,
        grad_input,
        outs[0].reshape(-1, local_mid),
        outs[2],
        outs[1].reshape(-1, local_ch),
    )


def solution(mesh):
    rows, channels = mesh.devices.shape
    fine = Mesh(mesh.devices.reshape(rows, channels // 2, 2), ("row", "z", "core"))
    ch = ("z", "core")
    placed = (
        P("row", None, ch),
        P(None, ch),
        P(None, None, None, ch),
        P(None, ch),
        P("row", None, ch),
    )
    return jax.shard_map(
        body,
        mesh=fine,
        in_specs=placed,
        out_specs=(
            P("row", None, ch),
            P("row", None, ch),
            P(None, ch),
            P(None, None, None, ch),
            P(None, ch),
        ),
        check_vma=False,
    )
```
